128 devices in a mesh: member: 32 (over y, x, core), space: 4 (over z).
Axes of the slice: x: 4, y: 4, z: 4, core: 2. Of those that a mesh axis runs over, the one named last changes fastest.
Arguments:
- background: bfloat16 [256, 4, 65536], P('member', None, 'space'), may hold values from -6 to 6
- obs_ens: float32 [256, 32768], P('member', 'space'), may hold values from -6 to 6
- observed: float32 [32768], P('space'), may hold values from -8 to 8
- variance: float32 [32768], P('space'), may hold values from 0.5 to 4
- obs_slot: int32 [4, 64, 512], P('space', 'member'), may hold values from 0 to 24575
- obs_count: int32 [4, 64], P('space', 'member'), may hold values from 256 to 512
- loc_bin: int32 [4, 64, 512], P('space', 'member'), may hold values from 0 to 31
Outputs:
- analysis: bfloat16 [256, 4, 65536], P('member', None, 'space')
The draws below stay inside these ranges and needn't reach their ends.
All inputs are finite; a program needn't handle non-finite values.
Results may differ from the reference program's by a relative error of at most 0.0056.
Values may be sent and summed in bfloat16 or wider, within the bound.
No kernel may reach another device: no remote copies, remote signals or barrier semaphores. Data moves between devices by JAX's collectives and lax.ppermute only.
A program may use at most 192 MiB of HBM per device.

```python
import math
import jax
import jax.numpy as jnp
from jax import lax

K = 256
L = 4
OBS_LOC = 512
OBS_TILE = 8192
ITERS = 8
NBINS = 32
NTILE = 4
BLK_TILE = 64
NCOL = 65536
NOBS = 32768


def draw_obs_slot(key, part):
    top_value = 3 * OBS_TILE
    entries = NTILE * BLK_TILE * OBS_LOC
    key_vals, key_spot = jax.random.split(key, 2)
    values = jax.random.randint(key_vals, (entries,), 0, top_value, dtype=jnp.int32)
    spot_one = jax.random.randint(key_spot, (), 0, entries, dtype=jnp.int32)
    spot_two = (spot_one + 1) % entries
    values = values.at[spot_one].set(top_value - 1)
    values = values.at[spot_two].set(0)
    return values.reshape(NTILE, BLK_TILE, OBS_LOC)


def draw_obs_count(key, part):
    entries = NTILE * BLK_TILE
    key_vals, key_spot = jax.random.split(jax.random.fold_in(key, 7), 2)
    values = jax.random.randint(key_vals, (entries,), OBS_LOC // 2, OBS_LOC + 1, dtype=jnp.int32)
    spot_one = jax.random.randint(key_spot, (), 0, entries, dtype=jnp.int32)
    spot_two = (spot_one + 1) % entries
    values = values.at[spot_one].set(OBS_LOC)
    values = values.at[spot_two].set(OBS_LOC // 2)
    return values.reshape(NTILE, BLK_TILE)


def with_ends(array, key, low, largest):
    extent = array.shape
    index_at = [jax.random.randint(jax.random.fold_in(key, axis), (), 0, extent[axis]) for axis in range(len(extent))]
    array = array.at[tuple(index_at)].set(low)
    longest = extent.index(max(extent))
    index_at[longest] = (index_at[longest] + 1) % extent[longest]
    return array.at[tuple(index_at)].set(largest)


def shard_levels(rng, shape, cuts, low, high):
    level, own = 1.0, jax.random.fold_in(rng, 6)
    for position, shards_of in cuts:
        heights = jnp.exp(jax.random.uniform(jax.random.fold_in(own, position), (shards_of,), jnp.float32, low / len(cuts), high / len(cuts)))
        level = level * jnp.repeat(heights, shape[position] // shards_of).reshape([-1 if axis == position else 1 for axis in range(len(shape))])
    return level


def normal_values(stream_key, extent, scale, limit, cuts=(), kind=jnp.bfloat16):
    values = scale * jax.random.normal(stream_key, extent, jnp.float32)
    if cuts:
        values = values * shard_levels(stream_key, extent, cuts, -0.22, 0.18)
    return jnp.clip(values, -limit, limit).astype(kind)


def setup_inputs(seed: int = 0) -> dict:
    splits = jax.random.split(jax.random.key(seed), 8)
    background = normal_values(splits[0], (K, L, NCOL), 1.0, 6.0, ((0, 32), (2, 4)))
    obs_ens = normal_values(splits[1], (K, NOBS), 1.0, 6.0, ((0, 32), (1, 4)), jnp.float32)
    observed = normal_values(splits[2], (NOBS,), 2.0, 8.0, ((0, 4),), jnp.float32)
    variance = jnp.clip(jnp.exp(math.log(4.0) - 2.0794415 * jax.random.uniform(splits[3], (NOBS,), jnp.float32) ** shard_levels(splits[3], (NOBS,), ((0, 4),), -0.2, 0.2)), 0.5, 4.0)
    obs_slot = draw_obs_slot(jax.random.fold_in(splits[7], 71), 0)
    obs_count = draw_obs_count(jax.random.fold_in(splits[7], 71), 0)
    loc_bin = with_ends(jax.random.randint(splits[6], (NTILE, BLK_TILE, OBS_LOC), 0, NBINS), jax.random.fold_in(splits[6], 1), 0, NBINS - 1).astype(jnp.int32)
    return {"background": background, "obs_ens": obs_ens, "observed": observed, "variance": variance, "obs_slot": obs_slot, "obs_count": obs_count, "loc_bin": loc_bin}


def localize(bin_idx):
    scaled = bin_idx.astype(jnp.float32) / (NBINS * 0.375)
    return jnp.exp(-0.5 * scaled * scaled)

def transforms(columns, departure, weight):
    members = columns.shape[0]
    highest = lax.Precision.HIGHEST
    scaled = columns * weight[None]
    gram_mat = jnp.einsum('kbp,jbp->bkj', scaled, columns, precision=highest)
    identity = jnp.eye(members, dtype=jnp.float32)
    system = gram_mat + (members - 1.0) * identity[None]
    half_trace = 0.5 * jnp.trace(system, axis1=1, axis2=2)
    root_iter = system / half_trace[:, None, None]
    inv_root = jnp.broadcast_to(identity[None], root_iter.shape)
    for sweep_num in range(ITERS):
        correct = 1.5 * identity[None] - 0.5 * jnp.einsum('bij,bjk->bik', inv_root, root_iter, precision=highest)
        root_iter = jnp.einsum('bij,bjk->bik', root_iter, correct, precision=highest)
        inv_root = jnp.einsum('bij,bjk->bik', correct, inv_root, precision=highest)
    covariance = jnp.einsum('bij,bjk->bik', inv_root, inv_root, precision=highest) / half_trace[:, None, None]
    pulled = jnp.einsum('kbp,bp->bk', scaled, departure, precision=highest)
    mean_shift = jnp.einsum('bij,bj->bi', covariance, pulled, precision=highest)
    spread = inv_root * jnp.sqrt((members - 1.0) / half_trace)[:, None, None]
    return (spread + mean_shift[:, :, None]).astype(jnp.bfloat16)

def analyse(columns, weights_tot):
    members, levels, span_cols = columns.shape
    blocks = weights_tot.shape[0]
    average = lax.optimization_barrier(jnp.mean(columns.astype(jnp.float32), axis=0))
    perturb = (columns.astype(jnp.float32) - average[None]).astype(jnp.bfloat16)
    blocked = perturb.reshape(members, levels, blocks, span_cols // blocks)
    increment = jnp.einsum('klbc,bkn->nlbc', blocked.astype(jnp.float32), weights_tot.astype(jnp.float32), precision=lax.Precision.HIGHEST)
    return (increment.reshape(members, levels, span_cols) + average[None]).astype(jnp.bfloat16)

def reference(background, obs_ens, observed, variance, obs_slot, obs_count, loc_bin):
    tile_count = obs_slot.shape[0]
    members, levels, col_total = background.shape
    tile_obs = observed.shape[0] // tile_count
    tile_cols = col_total // tile_count
    obs_mean = lax.optimization_barrier(jnp.mean(obs_ens, axis=0))
    obs_pert = obs_ens - obs_mean[None]
    departure = observed - obs_mean
    field_view = background.reshape(members, levels, tile_count, tile_cols)

    def one_tile(tile_num):
        slot_idx = lax.dynamic_index_in_dim(obs_slot, tile_num, 0, keepdims=False)
        counts = lax.dynamic_index_in_dim(obs_count, tile_num, 0, keepdims=False)
        bin_idx = lax.dynamic_index_in_dim(loc_bin, tile_num, 0, keepdims=False)
        source = (tile_num - 1 + slot_idx // tile_obs) % tile_count
        global_idx = (source * tile_obs + slot_idx % tile_obs).astype(jnp.int32)
        columns = jnp.take(obs_pert, global_idx, axis=1)
        in_range = jnp.arange(slot_idx.shape[1], dtype=jnp.int32)[None, :] < counts[:, None]
        weight = jnp.where(in_range, localize(bin_idx) / variance[global_idx], 0.0)
        weights_tot = transforms(columns, departure[global_idx], weight)
        fields = lax.dynamic_index_in_dim(field_view, tile_num, 2, keepdims=False)
        return analyse(fields, weights_tot)
    result = lax.map(one_tile, jnp.arange(tile_count, dtype=jnp.int32))
    return jnp.moveaxis(result, 0, 2).reshape(members, levels, col_total)
```

```python
import jax
import jax.numpy as jnp
from jax import lax
from jax.sharding import Mesh, PartitionSpec as P

ITERS = 8
NBINS = 32
GROUP = 8
MEMBER = ("my", "mx")


def localize(bin_idx):
    scaled = bin_idx.astype(jnp.float32) / (NBINS * 0.375)
    return jnp.exp(-0.5 * scaled * scaled)


def transforms(cols_t, departure, weight):
    members = cols_t.shape[2]
    highest = lax.Precision.HIGHEST
    scaled = cols_t * weight[:, :, None]
    gram_mat = jnp.einsum("bpk,bpj->bkj", scaled, cols_t, precision=highest)
    identity = jnp.eye(members, dtype=jnp.float32)
    system = gram_mat + (members - 1.0) * identity[None]
    half_trace = 0.5 * jnp.trace(system, axis1=1, axis2=2)
    root_iter = system / half_trace[:, None, None]
    inv_root = jnp.broadcast_to(identity[None], root_iter.shape)
    for sweep_num in range(ITERS):
        correct = 1.5 * identity[None] - 0.5 * jnp.einsum(
            "bij,bjk->bik", inv_root, root_iter, precision=highest
        )
        root_iter = jnp.einsum("bij,bjk->bik", root_iter, correct, precision=highest)
        inv_root = jnp.einsum("bij,bjk->bik", correct, inv_root, precision=highest)
    covariance = (
        jnp.einsum("bij,bjk->bik", inv_root, inv_root, precision=highest)
        / half_trace[:, None, None]
    )
    pulled = jnp.einsum("bpk,bp->bk", scaled, departure, precision=highest)
    mean_shift = jnp.einsum("bij,bj->bi", covariance, pulled, precision=highest)
    spread = inv_root * jnp.sqrt((members - 1.0) / half_trace)[:, None, None]
    return (spread + mean_shift[:, :, None]).astype(jnp.bfloat16)


def analyse(fields, weights_tot):
    members, levels, span_cols = fields.shape
    blocks = weights_tot.shape[0]
    average = jnp.mean(fields.astype(jnp.float32), axis=0)
    perturb = (fields.astype(jnp.float32) - average[None]).astype(jnp.bfloat16)
    blocked = perturb.reshape(members, levels, blocks, span_cols // blocks)
    increment = jnp.einsum(
        "klbc,bkn->nlbc", blocked, weights_tot, preferred_element_type=jnp.float32
    )
    return (increment.reshape(members, levels, span_cols) + average[None]).astype(jnp.bfloat16)


def per_device(background, obs_ens, observed, variance, obs_slot, obs_count, loc_bin):
    n_y = lax.axis_size("my")
    n_x = lax.axis_size("mx")
    n_m = n_y * n_x
    n_s = lax.axis_size("space")
    k_loc, levels, span = background.shape
    members = k_loc * n_m
    chunk = span // n_m
    blk_loc, n_slot = obs_slot.shape[1], obs_slot.shape[2]

    send_bg = background.reshape(k_loc, levels, n_m, chunk).transpose(2, 0, 1, 3)
    fields = lax.all_to_all(send_bg, MEMBER, 0, 0, tiled=True).reshape(members, levels, chunk)

    rows = jnp.concatenate([obs_ens, observed[None], variance[None]], axis=0)
    up = [(i, (i + 1) % n_s) for i in range(n_s)]
    down = [((i + 1) % n_s, i) for i in range(n_s)]
    before = lax.ppermute(rows, "space", up)
    after = lax.ppermute(rows, "space", down)
    near = jnp.concatenate([before, rows, after], axis=1)
    side = near[k_loc:]

    group = lax.all_gather(near[:k_loc], "mx", axis=0, tiled=True)
    group_t = group.T

    slots_grp = lax.all_gather(obs_slot[0], "my", axis=0, tiled=True)
    picked = jnp.take(group_t, slots_grp.reshape(-1), axis=0)
    send = picked.reshape(n_y, blk_loc * n_slot, n_x * k_loc)
    recv = lax.all_to_all(send, "my", 0, 0, tiled=True)
    ens_cols = recv.transpose(1, 0, 2).reshape(blk_loc, n_slot, members)

    obs_mean = jnp.mean(ens_cols, axis=2)
    cols_t = ens_cols - obs_mean[:, :, None]
    side_cols = jnp.take(side, obs_slot[0].reshape(-1), axis=1).reshape(2, blk_loc, n_slot)
    dep_cols = side_cols[0] - obs_mean
    var_cols = side_cols[1]
    in_range = jnp.arange(n_slot, dtype=jnp.int32)[None, :] < obs_count[0][:, None]
    weight = jnp.where(in_range, localize(loc_bin[0]) / var_cols, 0.0)
    weights_tot = transforms(cols_t, dep_cols, weight)

    out = analyse(fields, weights_tot)
    send_out = out.reshape(n_m, k_loc, levels, chunk)
    back = lax.all_to_all(send_out, MEMBER, 0, 0, tiled=True)
    return back.transpose(1, 2, 0, 3).reshape(k_loc, levels, span)


def solution(mesh):
    devs = mesh.devices
    n_m, n_s = devs.shape
    mesh3 = Mesh(devs.reshape(n_m // GROUP, GROUP, n_s), ("my", "mx", "space"))
    in_specs = (
        P(MEMBER, None, "space"),
        P(MEMBER, "space"),
        P("space"),
        P("space"),
        P("space", MEMBER, None),
        P("space", MEMBER),
        P("space", MEMBER, None),
    )
    out_specs = P(MEMBER, None, "space")
    return jax.shard_map(
        per_device, mesh=mesh3, in_specs=in_specs, out_specs=out_specs, check_vma=False
    )
```

```python
import jax
import jax.numpy as jnp
from jax import lax
from jax.sharding import Mesh, PartitionSpec as P

ITERS = 8
NBINS = 32
MEMBER = ("my", "mx", "mc")


def localize(bin_idx):
    scaled = bin_idx.astype(jnp.float32) / (NBINS * 0.375)
    return jnp.exp(-0.5 * scaled * scaled)


def transforms(cols_t, departure, weight):
    members = cols_t.shape[2]
    highest = lax.Precision.HIGH
    scaled = cols_t * weight[:, :, None]
    gram_mat = jnp.einsum("bpk,bpj->bkj", scaled, cols_t, precision=highest)
    identity = jnp.eye(members, dtype=jnp.float32)
    system = gram_mat + (members - 1.0) * identity[None]
    half_trace = 0.5 * jnp.trace(system, axis1=1, axis2=2)
    root_iter = system / half_trace[:, None, None]
    inv_root = jnp.broadcast_to(identity[None], root_iter.shape)
    for sweep_num in range(ITERS):
        correct = 1.5 * identity[None] - 0.5 * jnp.einsum(
            "bij,bjk->bik", inv_root, root_iter, precision=highest
        )
        both = jnp.einsum(
            "bij,bjk->bik", correct, jnp.concatenate([root_iter, inv_root], axis=2),
            precision=highest,
        )
        root_iter, inv_root = both[:, :, :members], both[:, :, members:]
    covariance = (
        jnp.einsum("bij,bjk->bik", inv_root, inv_root, precision=highest)
        / half_trace[:, None, None]
    )
    pulled = jnp.einsum("bpk,bp->bk", scaled, departure, precision=highest)
    mean_shift = jnp.einsum("bij,bj->bi", covariance, pulled, precision=highest)
    spread = inv_root * jnp.sqrt((members - 1.0) / half_trace)[:, None, None]
    return (spread + mean_shift[:, :, None]).astype(jnp.bfloat16)


def analyse(fields, weights_tot):
    members, levels, span_cols = fields.shape
    blocks = weights_tot.shape[0]
    average = jnp.mean(fields.astype(jnp.float32), axis=0)
    perturb = (fields.astype(jnp.float32) - average[None]).astype(jnp.bfloat16)
    blocked = perturb.reshape(members, levels, blocks, span_cols // blocks)
    increment = jnp.einsum(
        "klbc,bkn->nlbc", blocked, weights_tot, preferred_element_type=jnp.float32
    )
    return (increment.reshape(members, levels, span_cols) + average[None]).astype(jnp.bfloat16)


def per_device(background, obs_ens, observed, variance, obs_slot, obs_count, loc_bin):
    n_y = lax.axis_size("my")
    n_x = lax.axis_size("mx")
    n_c = lax.axis_size("mc")
    n_m = n_y * n_x * n_c
    n_s = lax.axis_size("space")
    k_loc, levels, span = background.shape
    members = k_loc * n_m
    chunk = span // n_m
    blk_loc, n_slot = obs_slot.shape[1], obs_slot.shape[2]

    send_bg = background.reshape(k_loc, levels, n_m, chunk).transpose(2, 0, 1, 3)
    fields = lax.all_to_all(send_bg, MEMBER, 0, 0, tiled=True).reshape(members, levels, chunk)

    me_y = lax.axis_index("my")
    slots_own = obs_slot[0].reshape(-1)
    shifted = [slots_own]
    for d in range(1, n_y):
        shifted.append(lax.ppermute(slots_own, "my", [(i, (i + d) % n_y) for i in range(n_y)]))
    shifted = jnp.stack(shifted)
    slots_grp = jnp.take(shifted, (me_y - jnp.arange(n_y)) % n_y, axis=0)

    rows = jnp.concatenate([obs_ens, observed[None], variance[None]], axis=0)
    up = [(i, (i + 1) % n_s) for i in range(n_s)]
    down = [((i + 1) % n_s, i) for i in range(n_s)]
    before = lax.ppermute(rows, "space", up)
    after = lax.ppermute(rows, "space", down)
    near = jnp.concatenate([before, rows, after], axis=1)
    side = near[k_loc:]
    n_near = near.shape[1]

    half = lax.all_gather(near[:k_loc], "mx", axis=0, tiled=False)
    other = lax.ppermute(half, "mc", [(i, (i + 1) % n_c) for i in range(n_c)])
    me_c = lax.axis_index("mc")
    pair = jnp.where(me_c == 0, jnp.stack([half, other]), jnp.stack([other, half]))
    group_t = pair.transpose(3, 1, 0, 2).reshape(n_near, n_x * n_c * k_loc)

    picked = jnp.take(group_t, slots_grp.reshape(-1), axis=0)
    send = picked.reshape(n_y, blk_loc * n_slot, n_x * n_c * k_loc)
    recv = lax.all_to_all(send, "my", 0, 0, tiled=True)
    ens_cols = recv.transpose(1, 0, 2).reshape(blk_loc, n_slot, members)

    obs_mean = jnp.mean(ens_cols, axis=2)
    cols_t = ens_cols - obs_mean[:, :, None]
    side_cols = jnp.take(side, slots_own, axis=1).reshape(2, blk_loc, n_slot)
    dep_cols = side_cols[0] - obs_mean
    var_cols = side_cols[1]
    in_range = jnp.arange(n_slot, dtype=jnp.int32)[None, :] < obs_count[0][:, None]
    weight = jnp.where(in_range, localize(loc_bin[0]) / var_cols, 0.0)
    weights_tot = transforms(cols_t, dep_cols, weight)

    out = analyse(fields, weights_tot)
    send_out = out.reshape(n_m, k_loc, levels, chunk)
    back = lax.all_to_all(send_out, MEMBER, 0, 0, tiled=True)
    return back.transpose(1, 2, 0, 3).reshape(k_loc, levels, span)


def solution(mesh):
    devs = mesh.devices
    n_m, n_s = devs.shape
    n_c = 2
    n_y = n_m // (n_c * 4)
    mesh3 = Mesh(devs.reshape(n_y, n_m // (n_y * n_c), n_c, n_s), ("my", "mx", "mc", "space"))
    in_specs = (
        P(MEMBER, None, "space"),
        P(MEMBER, "space"),
        P("space"),
        P("space"),
        P("space", MEMBER, None),
        P("space", MEMBER),
        P("space", MEMBER, None),
    )
    out_specs = P(MEMBER, None, "space")
    return jax.shard_map(
        per_device, mesh=mesh3, in_specs=in_specs, out_specs=out_specs, check_vma=False
    )
```

```python
import jax
import jax.numpy as jnp
from jax import lax
from jax.sharding import Mesh, PartitionSpec as P

ITERS = 8
NBINS = 32
MEMBER = ("my", "mx", "mc")


def localize(bin_idx):
    scaled = bin_idx.astype(jnp.float32) / (NBINS * 0.375)
    return jnp.exp(-0.5 * scaled * scaled)


def transforms(cols_t, departure, weight):
    members = cols_t.shape[2]
    highest = lax.Precision.HIGH
    scaled = cols_t * weight[:, :, None]
    gram_mat = jnp.einsum("bpk,bpj->bkj", scaled, cols_t, precision=highest)
    identity = jnp.eye(members, dtype=jnp.float32)
    system = gram_mat + (members - 1.0) * identity[None]
    half_trace = 0.5 * jnp.trace(system, axis1=1, axis2=2)
    root_iter = system / half_trace[:, None, None]
    inv_root = jnp.broadcast_to(identity[None], root_iter.shape)
    for sweep_num in range(ITERS):
        correct = 1.5 * identity[None] - 0.5 * jnp.einsum(
            "bij,bjk->bik", inv_root, root_iter, precision=highest
        )
        both = jnp.einsum(
            "bij,bjk->bik", correct, jnp.concatenate([root_iter, inv_root], axis=2),
            precision=highest,
        )
        root_iter, inv_root = both[:, :, :members], both[:, :, members:]
    covariance = (
        jnp.einsum("bij,bjk->bik", inv_root, inv_root, precision=highest)
        / half_trace[:, None, None]
    )
    pulled = jnp.einsum("bpk,bp->bk", scaled, departure, precision=highest)
    mean_shift = jnp.einsum("bij,bj->bi", covariance, pulled, precision=highest)
    spread = inv_root * jnp.sqrt((members - 1.0) / half_trace)[:, None, None]
    return (spread + mean_shift[:, :, None]).astype(jnp.bfloat16)


def analyse(fields, weights_tot):
    members, levels, span_cols = fields.shape
    blocks = weights_tot.shape[0]
    average = jnp.mean(fields.astype(jnp.float32), axis=0)
    perturb = (fields.astype(jnp.float32) - average[None]).astype(jnp.bfloat16)
    blocked = perturb.reshape(members, levels, blocks, span_cols // blocks)
    increment = jnp.einsum(
        "klbc,bkn->nlbc", blocked, weights_tot, preferred_element_type=jnp.float32
    )
    return (increment.reshape(members, levels, span_cols) + average[None]).astype(jnp.bfloat16)


def per_device(background, obs_ens, observed, variance, obs_slot, obs_count, loc_bin):
    n_y = lax.axis_size("my")
    n_x = lax.axis_size("mx")
    n_c = lax.axis_size("mc")
    n_m = n_y * n_x * n_c
    n_s = lax.axis_size("space")
    k_loc, levels, span = background.shape
    members = k_loc * n_m
    chunk = span // n_m
    blk_loc, n_slot = obs_slot.shape[1], obs_slot.shape[2]

    send_bg = background.reshape(k_loc, levels, n_m, chunk).transpose(2, 0, 1, 3)
    fields = lax.all_to_all(send_bg, MEMBER, 0, 0, tiled=True).reshape(members, levels, chunk)

    me_y = lax.axis_index("my")
    slots_own = obs_slot[0].reshape(-1)
    shifted = [slots_own]
    for d in range(1, n_y):
        shifted.append(lax.ppermute(slots_own, "my", [(i, (i + d) % n_y) for i in range(n_y)]))
    shifted = jnp.stack(shifted)
    slots_grp = jnp.take(shifted, (me_y - jnp.arange(n_y)) % n_y, axis=0)

    rows = jnp.concatenate([obs_ens, observed[None], variance[None]], axis=0)
    up = [(i, (i + 1) % n_s) for i in range(n_s)]
    down = [((i + 1) % n_s, i) for i in range(n_s)]
    before = lax.ppermute(rows, "space", up)
    after = lax.ppermute(rows, "space", down)
    near = jnp.concatenate([before, rows, after], axis=1)
    side = near[k_loc:]
    n_near = near.shape[1]

    group_t = lax.all_gather(near[:k_loc].T, ("mx", "mc"), axis=1, tiled=True)

    picked = jnp.take(group_t, slots_grp.reshape(-1), axis=0)
    send = picked.reshape(n_y, blk_loc * n_slot, n_x * n_c * k_loc)
    recv = lax.all_to_all(send, "my", 0, 0, tiled=True)
    ens_cols = recv.transpose(1, 0, 2).reshape(blk_loc, n_slot, members)

    obs_mean = jnp.mean(ens_cols, axis=2)
    cols_t = ens_cols - obs_mean[:, :, None]
    side_cols = jnp.take(side, slots_own, axis=1).reshape(2, blk_loc, n_slot)
    dep_cols = side_cols[0] - obs_mean
    var_cols = side_cols[1]
    in_range = jnp.arange(n_slot, dtype=jnp.int32)[None, :] < obs_count[0][:, None]
    weight = jnp.where(in_range, localize(loc_bin[0]) / var_cols, 0.0)
    weights_tot = transforms(cols_t, dep_cols, weight)

    out = analyse(fields, weights_tot)
    send_out = out.reshape(n_m, k_loc, levels, chunk)
    back = lax.all_to_all(send_out, MEMBER, 0, 0, tiled=True)
    return back.transpose(1, 2, 0, 3).reshape(k_loc, levels, span)


def solution(mesh):
    devs = mesh.devices
    n_m, n_s = devs.shape
    n_c = 2
    n_y = n_m // (n_c * 4)
    mesh3 = Mesh(devs.reshape(n_y, n_m // (n_y * n_c), n_c, n_s), ("my", "mx", "mc", "space"))
    in_specs = (
        P(MEMBER, None, "space"),
        P(MEMBER, "space"),
        P("space"),
        P("space"),
        P("space", MEMBER, None),
        P("space", MEMBER),
        P("space", MEMBER, None),
    )
    out_specs = P(MEMBER, None, "space")
    return jax.shard_map(
        per_device, mesh=mesh3, in_specs=in_specs, out_specs=out_specs, check_vma=False
    )
```

```python
import jax
import jax.numpy as jnp
from jax import lax
from jax.sharding import Mesh, PartitionSpec as P

ITERS = 8
NBINS = 32
MEMBER = ("my", "mx", "mc")


def localize(bin_idx):
    scaled = bin_idx.astype(jnp.float32) / (NBINS * 0.375)
    return jnp.exp(-0.5 * scaled * scaled)


def transforms(cols_t, departure, weight):
    members = cols_t.shape[2]
    highest = lax.Precision.HIGH
    scaled = cols_t * weight[:, :, None]
    gram_mat = jnp.einsum("bpk,bpj->bkj", scaled, cols_t, precision=highest)
    identity = jnp.eye(members, dtype=jnp.float32)
    system = gram_mat + (members - 1.0) * identity[None]
    half_trace = 0.5 * jnp.trace(system, axis1=1, axis2=2)
    root_iter = system / half_trace[:, None, None]
    inv_root = jnp.broadcast_to(identity[None], root_iter.shape)
    for sweep_num in range(ITERS):
        correct = 1.5 * identity[None] - 0.5 * jnp.einsum(
            "bij,bjk->bik", inv_root, root_iter, precision=highest
        )
        both = jnp.einsum(
            "bij,bjk->bik", correct, jnp.concatenate([root_iter, inv_root], axis=2),
            precision=highest,
        )
        root_iter, inv_root = both[:, :, :members], both[:, :, members:]
    covariance = (
        jnp.einsum("bij,bjk->bik", inv_root, inv_root, precision=highest)
        / half_trace[:, None, None]
    )
    pulled = jnp.einsum("bpk,bp->bk", scaled, departure, precision=highest)
    mean_shift = jnp.einsum("bij,bj->bi", covariance, pulled, precision=highest)
    spread = inv_root * jnp.sqrt((members - 1.0) / half_trace)[:, None, None]
    return (spread + mean_shift[:, :, None]).astype(jnp.bfloat16)


def analyse(fields, weights_tot, n_dest):
    members, levels, span_cols = fields.shape
    blocks = weights_tot.shape[0]
    average = jnp.mean(fields.astype(jnp.float32), axis=0)
    perturb = (fields.astype(jnp.float32) - average[None]).astype(jnp.bfloat16)
    blocked = perturb.reshape(members, levels, blocks, span_cols // blocks)
    w_split = weights_tot.reshape(blocks, members, n_dest, members // n_dest)
    increment = jnp.einsum(
        "klbc,bkdn->dnlbc", blocked, w_split, preferred_element_type=jnp.float32
    )
    increment = increment.reshape(n_dest, members // n_dest, levels, span_cols)
    return (increment + average[None, None]).astype(jnp.bfloat16)


def per_device(background, obs_ens, observed, variance, obs_slot, obs_count, loc_bin):
    n_y = lax.axis_size("my")
    n_x = lax.axis_size("mx")
    n_c = lax.axis_size("mc")
    n_m = n_y * n_x * n_c
    n_s = lax.axis_size("space")
    k_loc, levels, span = background.shape
    members = k_loc * n_m
    chunk = span // n_m
    blk_loc, n_slot = obs_slot.shape[1], obs_slot.shape[2]

    send_bg = background.reshape(k_loc, levels, n_m, chunk).transpose(2, 0, 1, 3)

    me_y = lax.axis_index("my")
    slots_own = obs_slot[0].reshape(-1)
    shifted = [slots_own]
    for d in range(1, n_y):
        shifted.append(lax.ppermute(slots_own, "my", [(i, (i + d) % n_y) for i in range(n_y)]))
    shifted = jnp.stack(shifted)
    slots_grp = jnp.take(shifted, (me_y - jnp.arange(n_y)) % n_y, axis=0)

    rows = jnp.concatenate([obs_ens, observed[None], variance[None]], axis=0)
    up = [(i, (i + 1) % n_s) for i in range(n_s)]
    down = [((i + 1) % n_s, i) for i in range(n_s)]
    before = lax.ppermute(rows, "space", up)
    after = lax.ppermute(rows, "space", down)
    near = jnp.concatenate([before, rows, after], axis=1)
    side = near[k_loc:]
    n_near = near.shape[1]

    group_t = lax.all_gather(near[:k_loc].T, ("mx", "mc"), axis=1, tiled=True)

    group_t, send_bg = lax.optimization_barrier((group_t, send_bg))
    fields = lax.all_to_all(send_bg, MEMBER, 0, 0, tiled=True).reshape(members, levels, chunk)

    picked = jnp.take(group_t, slots_grp.reshape(-1), axis=0)
    picked, fields = lax.optimization_barrier((picked, fields))
    send = picked.reshape(n_y, blk_loc * n_slot, n_x * n_c * k_loc)
    recv = lax.all_to_all(send, "my", 0, 0, tiled=True)
    ens_cols = recv.transpose(1, 0, 2).reshape(blk_loc, n_slot, members)

    obs_mean = jnp.mean(ens_cols, axis=2)
    cols_t = ens_cols - obs_mean[:, :, None]
    side_cols = jnp.take(side, slots_own, axis=1).reshape(2, blk_loc, n_slot)
    dep_cols = side_cols[0] - obs_mean
    var_cols = side_cols[1]
    in_range = jnp.arange(n_slot, dtype=jnp.int32)[None, :] < obs_count[0][:, None]
    weight = jnp.where(in_range, localize(loc_bin[0]) / var_cols, 0.0)
    weights_tot = transforms(cols_t, dep_cols, weight)

    send_out = analyse(fields, weights_tot, n_m)
    back = lax.all_to_all(send_out, MEMBER, 0, 0, tiled=True)
    return back.transpose(1, 2, 0, 3).reshape(k_loc, levels, span)


def solution(mesh):
    devs = mesh.devices
    n_m, n_s = devs.shape
    n_c = 2
    n_y = n_m // (n_c * 4)
    mesh3 = Mesh(devs.reshape(n_y, n_m // (n_y * n_c), n_c, n_s), ("my", "mx", "mc", "space"))
    in_specs = (
        P(MEMBER, None, "space"),
        P(MEMBER, "space"),
        P("space"),
        P("space"),
        P("space", MEMBER, None),
        P("space", MEMBER),
        P("space", MEMBER, None),
    )
    out_specs = P(MEMBER, None, "space")
    return jax.shard_map(
        per_device, mesh=mesh3, in_specs=in_specs, out_specs=out_specs, check_vma=False
    )
```

```python
import jax
import jax.numpy as jnp
from jax import lax
from jax.sharding import Mesh, PartitionSpec as P

ITERS = 8
NBINS = 32
MEMBER = ("my", "mx", "mc")


def localize(bin_idx):
    scaled = bin_idx.astype(jnp.float32) / (NBINS * 0.375)
    return jnp.exp(-0.5 * scaled * scaled)


def transforms(cols_t, departure, weight):
    members = cols_t.shape[2]
    highest = lax.Precision.HIGH
    scaled = cols_t * weight[:, :, None]
    gram_mat = jnp.einsum("bpk,bpj->bkj", scaled, cols_t, precision=highest)
    identity = jnp.eye(members, dtype=jnp.float32)
    system = gram_mat + (members - 1.0) * identity[None]
    half_trace = 0.5 * jnp.trace(system, axis1=1, axis2=2)
    root_iter = system / half_trace[:, None, None]
    inv_root = jnp.broadcast_to(identity[None], root_iter.shape)
    for sweep_num in range(ITERS):
        correct = 1.5 * identity[None] - 0.5 * jnp.einsum(
            "bij,bjk->bik", inv_root, root_iter, precision=highest
        )
        both = jnp.einsum(
            "bij,bjk->bik", correct, jnp.concatenate([root_iter, inv_root], axis=2),
            precision=highest,
        )
        root_iter, inv_root = both[:, :, :members], both[:, :, members:]
    covariance = (
        jnp.einsum("bij,bjk->bik", inv_root, inv_root, precision=highest)
        / half_trace[:, None, None]
    )
    pulled = jnp.einsum("bpk,bp->bk", scaled, departure, precision=highest)
    mean_shift = jnp.einsum("bij,bj->bi", covariance, pulled, precision=highest)
    spread = inv_root * jnp.sqrt((members - 1.0) / half_trace)[:, None, None]
    return (spread + mean_shift[:, :, None]).astype(jnp.bfloat16)


def analyse(fields, weights_tot, n_dest):
    members, levels, span_cols = fields.shape
    blocks = weights_tot.shape[0]
    average = jnp.mean(fields.astype(jnp.float32), axis=0)
    perturb = (fields.astype(jnp.float32) - average[None]).astype(jnp.bfloat16)
    blocked = perturb.reshape(members, levels, blocks, span_cols // blocks)
    w_split = weights_tot.reshape(blocks, members, n_dest, members // n_dest)
    increment = jnp.einsum(
        "klbc,bkdn->dnlbc", blocked, w_split, preferred_element_type=jnp.float32
    )
    increment = increment.reshape(n_dest, members // n_dest, levels, span_cols)
    return (increment + average[None, None]).astype(jnp.bfloat16)


def per_device(background, obs_ens, observed, variance, obs_slot, obs_count, loc_bin):
    n_y = lax.axis_size("my")
    n_x = lax.axis_size("mx")
    n_c = lax.axis_size("mc")
    n_m = n_y * n_x * n_c
    n_s = lax.axis_size("space")
    k_loc, levels, span = background.shape
    members = k_loc * n_m
    chunk = span // n_m
    blk_loc, n_slot = obs_slot.shape[1], obs_slot.shape[2]

    send_bg = background.reshape(k_loc, levels, n_m, chunk).transpose(2, 0, 1, 3)

    me_y = lax.axis_index("my")
    slots_own = obs_slot[0].reshape(-1)
    shifted = [slots_own]
    for d in range(1, n_y):
        shifted.append(lax.ppermute(slots_own, "my", [(i, (i + d) % n_y) for i in range(n_y)]))
    shifted = jnp.stack(shifted)
    slots_grp = shifted.at[(me_y - jnp.arange(n_y)) % n_y].get(mode="promise_in_bounds")

    rows = jnp.concatenate([obs_ens, observed[None], variance[None]], axis=0)
    up = [(i, (i + 1) % n_s) for i in range(n_s)]
    down = [((i + 1) % n_s, i) for i in range(n_s)]
    before = lax.ppermute(rows, "space", up)
    after = lax.ppermute(rows, "space", down)
    near = jnp.concatenate([before, rows, after], axis=1)
    side = near[k_loc:]
    n_near = near.shape[1]

    group_t = lax.all_gather(near[:k_loc].T, ("mx", "mc"), axis=1, tiled=True)

    group_t, send_bg = lax.optimization_barrier((group_t, send_bg))
    fields = lax.all_to_all(send_bg, MEMBER, 0, 0, tiled=True).reshape(members, levels, chunk)

    picked = group_t.at[slots_grp.reshape(-1)].get(mode="promise_in_bounds")
    picked, fields = lax.optimization_barrier((picked, fields))
    send = picked.reshape(n_y, blk_loc * n_slot, n_x * n_c * k_loc)
    recv = lax.all_to_all(send, "my", 0, 0, tiled=True)
    ens_cols = recv.transpose(1, 0, 2).reshape(blk_loc, n_slot, members)

    obs_mean = jnp.mean(ens_cols, axis=2)
    cols_t = ens_cols - obs_mean[:, :, None]
    side_cols = side.at[:, slots_own].get(mode="promise_in_bounds").reshape(2, blk_loc, n_slot)
    dep_cols = side_cols[0] - obs_mean
    var_cols = side_cols[1]
    in_range = jnp.arange(n_slot, dtype=jnp.int32)[None, :] < obs_count[0][:, None]
    weight = jnp.where(in_range, localize(loc_bin[0]) / var_cols, 0.0)
    weights_tot = transforms(cols_t, dep_cols, weight)

    send_out = analyse(fields, weights_tot, n_m)
    back = lax.all_to_all(send_out, MEMBER, 0, 0, tiled=True)
    return back.transpose(1, 2, 0, 3).reshape(k_loc, levels, span)


def solution(mesh):
    devs = mesh.devices
    n_m, n_s = devs.shape
    n_c = 2
    n_y = n_m // (n_c * 4)
    mesh3 = Mesh(devs.reshape(n_y, n_m // (n_y * n_c), n_c, n_s), ("my", "mx", "mc", "space"))
    in_specs = (
        P(MEMBER, None, "space"),
        P(MEMBER, "space"),
        P("space"),
        P("space"),
        P("space", MEMBER, None),
        P("space", MEMBER),
        P("space", MEMBER, None),
    )
    out_specs = P(MEMBER, None, "space")
    return jax.shard_map(
        per_device, mesh=mesh3, in_specs=in_specs, out_specs=out_specs, check_vma=False
    )
```

```python
import jax
import jax.numpy as jnp
from jax import lax
from jax.sharding import Mesh, PartitionSpec as P

ITERS = 8
NBINS = 32
MEMBER = ("my", "mx", "mc")


def localize(bin_idx):
    scaled = bin_idx.astype(jnp.float32) / (NBINS * 0.375)
    return jnp.exp(-0.5 * scaled * scaled)


def transforms(cols_t, departure, weight):
    members = cols_t.shape[2]
    highest = lax.Precision.HIGH
    scaled = cols_t * weight[:, :, None]
    gram_mat = jnp.einsum("bpk,bpj->bkj", scaled, cols_t, precision=highest)
    identity = jnp.eye(members, dtype=jnp.float32)
    system = gram_mat + (members - 1.0) * identity[None]
    half_trace = 0.5 * jnp.trace(system, axis1=1, axis2=2)
    root_iter = system / half_trace[:, None, None]
    inv_root = jnp.broadcast_to(identity[None], root_iter.shape)
    for sweep_num in range(ITERS):
        correct = 1.5 * identity[None] - 0.5 * jnp.einsum(
            "bij,bjk->bik", inv_root, root_iter, precision=highest
        )
        both = jnp.einsum(
            "bij,bjk->bik", correct, jnp.concatenate([root_iter, inv_root], axis=2),
            precision=highest,
        )
        root_iter, inv_root = both[:, :, :members], both[:, :, members:]
    covariance = (
        jnp.einsum("bij,bjk->bik", inv_root, inv_root, precision=highest)
        / half_trace[:, None, None]
    )
    pulled = jnp.einsum("bpk,bp->bk", scaled, departure, precision=highest)
    mean_shift = jnp.einsum("bij,bj->bi", covariance, pulled, precision=highest)
    spread = inv_root * jnp.sqrt((members - 1.0) / half_trace)[:, None, None]
    return (spread + mean_shift[:, :, None]).astype(jnp.bfloat16)


def analyse(fields, weights_tot, n_dest):
    members, levels, span_cols = fields.shape
    blocks = weights_tot.shape[0]
    average = jnp.mean(fields.astype(jnp.float32), axis=0)
    perturb = (fields.astype(jnp.float32) - average[None]).astype(jnp.bfloat16)
    blocked = perturb.reshape(members, levels, blocks, span_cols // blocks)
    w_split = weights_tot.reshape(blocks, members, n_dest, members // n_dest)
    increment = jnp.einsum(
        "klbc,bkdn->dnlbc", blocked, w_split, preferred_element_type=jnp.float32
    )
    increment = increment.reshape(n_dest, members // n_dest, levels, span_cols)
    return (increment + average[None, None]).astype(jnp.bfloat16)


def per_device(background, obs_ens, observed, variance, obs_slot, obs_count, loc_bin):
    n_y = lax.axis_size("my")
    n_x = lax.axis_size("mx")
    n_c = lax.axis_size("mc")
    n_m = n_y * n_x * n_c
    n_s = lax.axis_size("space")
    k_loc, levels, span = background.shape
    members = k_loc * n_m
    chunk = span // n_m
    blk_loc, n_slot = obs_slot.shape[1], obs_slot.shape[2]

    send_bg = background.reshape(k_loc, levels, n_m, chunk).transpose(2, 0, 1, 3)

    me_y = lax.axis_index("my")
    slots_own = obs_slot[0].reshape(-1)
    shifted = [slots_own]
    for d in range(1, n_y):
        shifted.append(lax.ppermute(slots_own, "my", [(i, (i + d) % n_y) for i in range(n_y)]))
    shifted = jnp.stack(shifted)
    slots_grp = shifted.at[(me_y - jnp.arange(n_y)) % n_y].get(mode="promise_in_bounds")

    rows = jnp.concatenate([obs_ens, observed[None], variance[None]], axis=0)
    up = [(i, (i + 1) % n_s) for i in range(n_s)]
    down = [((i + 1) % n_s, i) for i in range(n_s)]
    before = lax.ppermute(rows, "space", up)
    after = lax.ppermute(rows, "space", down)
    near = jnp.concatenate([before, rows, after], axis=1)
    obs_cols = near[k_loc].at[slots_own].get(mode="promise_in_bounds").reshape(blk_loc, n_slot)
    var_cols = near[k_loc + 1].at[slots_own].get(mode="promise_in_bounds").reshape(blk_loc, n_slot)
    n_near = near.shape[1]

    group_t = lax.all_gather(near[:k_loc].T, ("mx", "mc"), axis=1, tiled=True)

    group_t, send_bg, obs_cols, var_cols = lax.optimization_barrier(
        (group_t, send_bg, obs_cols, var_cols)
    )
    fields = lax.all_to_all(send_bg, MEMBER, 0, 0, tiled=True).reshape(members, levels, chunk)

    picked = jnp.take(group_t, slots_grp.reshape(-1), axis=0, mode="clip")
    picked, fields = lax.optimization_barrier((picked, fields))
    send = picked.reshape(n_y, blk_loc * n_slot, n_x * n_c * k_loc)
    recv = lax.all_to_all(send, "my", 0, 0, tiled=True)
    ens_cols = recv.transpose(1, 0, 2).reshape(blk_loc, n_slot, members)

    obs_mean = jnp.mean(ens_cols, axis=2)
    cols_t = ens_cols - obs_mean[:, :, None]
    dep_cols = obs_cols - obs_mean
    in_range = jnp.arange(n_slot, dtype=jnp.int32)[None, :] < obs_count[0][:, None]
    weight = jnp.where(in_range, localize(loc_bin[0]) / var_cols, 0.0)
    weights_tot = transforms(cols_t, dep_cols, weight)

    send_out = analyse(fields, weights_tot, n_m)
    back = lax.all_to_all(send_out, MEMBER, 0, 0, tiled=True)
    return back.transpose(1, 2, 0, 3).reshape(k_loc, levels, span)


def solution(mesh):
    devs = mesh.devices
    n_m, n_s = devs.shape
    n_c = 2
    n_y = n_m // (n_c * 4)
    mesh3 = Mesh(devs.reshape(n_y, n_m // (n_y * n_c), n_c, n_s), ("my", "mx", "mc", "space"))
    in_specs = (
        P(MEMBER, None, "space"),
        P(MEMBER, "space"),
        P("space"),
        P("space"),
        P("space", MEMBER, None),
        P("space", MEMBER),
        P("space", MEMBER, None),
    )
    out_specs = P(MEMBER, None, "space")
    return jax.shard_map(
        per_device, mesh=mesh3, in_specs=in_specs, out_specs=out_specs, check_vma=False
    )
```

```python
import jax
import jax.numpy as jnp
from jax import lax
from jax.sharding import Mesh, PartitionSpec as P

ITERS = 8
NBINS = 32
MEMBER = ("my", "mx", "mc")


def localize(bin_idx):
    scaled = bin_idx.astype(jnp.float32) / (NBINS * 0.375)
    return jnp.exp(-0.5 * scaled * scaled)


def transforms(cols_t, departure, weight):
    members = cols_t.shape[2]
    highest = lax.Precision.HIGH
    scaled = cols_t * weight[:, :, None]
    gram_mat = jnp.einsum("bpk,bpj->bkj", scaled, cols_t, precision=highest)
    identity = jnp.eye(members, dtype=jnp.float32)
    system = gram_mat + (members - 1.0) * identity[None]
    half_trace = 0.5 * jnp.trace(system, axis1=1, axis2=2)
    root_iter = system / half_trace[:, None, None]
    correct = 1.5 * identity[None] - 0.5 * root_iter
    root_iter = jnp.einsum("bij,bjk->bik", correct, root_iter, precision=highest)
    inv_root = correct
    for sweep_num in range(1, ITERS):
        correct = 1.5 * identity[None] - 0.5 * jnp.einsum(
            "bij,bjk->bik", inv_root, root_iter, precision=highest
        )
        both = jnp.einsum(
            "bij,bjk->bik", correct, jnp.concatenate([root_iter, inv_root], axis=2),
            precision=highest,
        )
        root_iter, inv_root = both[:, :, :members], both[:, :, members:]
    covariance = (
        jnp.einsum("bij,bjk->bik", inv_root, inv_root, precision=highest)
        / half_trace[:, None, None]
    )
    pulled = jnp.einsum("bpk,bp->bk", scaled, departure, precision=highest)
    mean_shift = jnp.einsum("bij,bj->bi", covariance, pulled, precision=highest)
    spread = inv_root * jnp.sqrt((members - 1.0) / half_trace)[:, None, None]
    return (spread + mean_shift[:, :, None]).astype(jnp.bfloat16)


def analyse(fields, weights_tot, n_dest):
    members, levels, span_cols = fields.shape
    blocks = weights_tot.shape[0]
    average = jnp.mean(fields.astype(jnp.float32), axis=0)
    perturb = (fields.astype(jnp.float32) - average[None]).astype(jnp.bfloat16)
    blocked = perturb.reshape(members, levels, blocks, span_cols // blocks)
    w_split = weights_tot.reshape(blocks, members, n_dest, members // n_dest)
    increment = jnp.einsum(
        "klbc,bkdn->dnlbc", blocked, w_split, preferred_element_type=jnp.float32
    )
    increment = increment.reshape(n_dest, members // n_dest, levels, span_cols)
    return (increment + average[None, None]).astype(jnp.bfloat16)


def per_device(background, obs_ens, observed, variance, obs_slot, obs_count, loc_bin):
    n_y = lax.axis_size("my")
    n_x = lax.axis_size("mx")
    n_c = lax.axis_size("mc")
    n_m = n_y * n_x * n_c
    n_s = lax.axis_size("space")
    k_loc, levels, span = background.shape
    members = k_loc * n_m
    chunk = span // n_m
    blk_loc, n_slot = obs_slot.shape[1], obs_slot.shape[2]

    send_bg = background.reshape(k_loc, levels, n_m, chunk).transpose(2, 0, 1, 3)

    me_y = lax.axis_index("my")
    slots_own = obs_slot[0].reshape(-1)
    shifted = [slots_own]
    for d in range(1, n_y):
        shifted.append(lax.ppermute(slots_own, "my", [(i, (i + d) % n_y) for i in range(n_y)]))
    shifted = jnp.stack(shifted)
    slots_grp = shifted.at[(me_y - jnp.arange(n_y)) % n_y].get(mode="promise_in_bounds")

    rows = jnp.concatenate([obs_ens, observed[None], variance[None]], axis=0)
    up = [(i, (i + 1) % n_s) for i in range(n_s)]
    down = [((i + 1) % n_s, i) for i in range(n_s)]
    before = lax.ppermute(rows, "space", up)
    after = lax.ppermute(rows, "space", down)
    near = jnp.concatenate([before, rows, after], axis=1)
    obs_cols = near[k_loc].at[slots_own].get(mode="promise_in_bounds").reshape(blk_loc, n_slot)
    var_cols = near[k_loc + 1].at[slots_own].get(mode="promise_in_bounds").reshape(blk_loc, n_slot)
    n_near = near.shape[1]

    group_t = lax.all_gather(near[:k_loc].T, ("mx", "mc"), axis=1, tiled=True)

    obs_cols, var_cols, send_bg = lax.optimization_barrier((obs_cols, var_cols, send_bg))
    fields = lax.all_to_all(send_bg, MEMBER, 0, 0, tiled=True).reshape(members, levels, chunk)

    picked = jnp.take(group_t, slots_grp.reshape(-1), axis=0, mode="clip")
    picked, fields = lax.optimization_barrier((picked, fields))
    send = picked.reshape(n_y, blk_loc * n_slot, n_x * n_c * k_loc)
    recv = lax.all_to_all(send, "my", 0, 0, tiled=True)
    ens_cols = recv.transpose(1, 0, 2).reshape(blk_loc, n_slot, members)

    obs_mean = jnp.mean(ens_cols, axis=2)
    cols_t = ens_cols - obs_mean[:, :, None]
    dep_cols = obs_cols - obs_mean
    in_range = jnp.arange(n_slot, dtype=jnp.int32)[None, :] < obs_count[0][:, None]
    weight = jnp.where(in_range, localize(loc_bin[0]) / var_cols, 0.0)
    weights_tot = transforms(cols_t, dep_cols, weight)

    send_out = analyse(fields, weights_tot, n_m)
    back = lax.all_to_all(send_out, MEMBER, 0, 0, tiled=True)
    return back.transpose(1, 2, 0, 3).reshape(k_loc, levels, span)


def solution(mesh):
    devs = mesh.devices
    n_m, n_s = devs.shape
    n_c = 2
    n_y = n_m // (n_c * 4)
    mesh3 = Mesh(devs.reshape(n_y, n_m // (n_y * n_c), n_c, n_s), ("my", "mx", "mc", "space"))
    in_specs = (
        P(MEMBER, None, "space"),
        P(MEMBER, "space"),
        P("space"),
        P("space"),
        P("space", MEMBER, None),
        P("space", MEMBER),
        P("space", MEMBER, None),
    )
    out_specs = P(MEMBER, None, "space")
    return jax.shard_map(
        per_device, mesh=mesh3, in_specs=in_specs, out_specs=out_specs, check_vma=False
    )
```

```python
import jax
import jax.numpy as jnp
from jax import lax
from jax.sharding import Mesh, PartitionSpec as P
from jax.experimental import pallas as pl
from jax.experimental.pallas import tpu as pltpu

ITERS = 8
NBINS = 32
MEMBER = ("my", "mx", "mc")


def localize(bin_idx):
    scaled = bin_idx.astype(jnp.float32) / (NBINS * 0.375)
    return jnp.exp(-0.5 * scaled * scaled)


def _split_dot(p, q):
    p_hi = p.astype(jnp.bfloat16)
    p_lo = (p - p_hi.astype(jnp.float32)).astype(jnp.bfloat16)
    q_hi = q.astype(jnp.bfloat16)
    q_lo = (q - q_hi.astype(jnp.float32)).astype(jnp.bfloat16)
    out = jnp.dot(p_hi, q_hi, preferred_element_type=jnp.float32)
    out = out + jnp.dot(p_hi, q_lo, preferred_element_type=jnp.float32)
    return out + jnp.dot(p_lo, q_hi, preferred_element_type=jnp.float32)


def _ns_kernel(root_ref, inv_ref):
    size = root_ref.shape[1]
    rows = lax.broadcasted_iota(jnp.int32, (size, size), 0)
    cols = lax.broadcasted_iota(jnp.int32, (size, size), 1)
    eye = (rows == cols).astype(jnp.float32)
    root = root_ref[0]
    correct = 1.5 * eye - 0.5 * root
    root = _split_dot(correct, root)
    inv = correct
    for sweep_num in range(1, ITERS):
        correct = 1.5 * eye - 0.5 * _split_dot(inv, root)
        root = _split_dot(correct, root)
        inv = _split_dot(correct, inv)
    inv_ref[0] = inv


def newton_schulz(root_iter):
    blocks, size, _ = root_iter.shape
    spec = pl.BlockSpec((1, size, size), lambda b: (b, 0, 0))
    flops = blocks * (ITERS * 3 - 1) * 3 * 2 * size ** 3
    return pl.pallas_call(
        _ns_kernel,
        out_shape=jax.ShapeDtypeStruct(root_iter.shape, jnp.float32),
        grid=(blocks,),
        in_specs=[spec],
        out_specs=spec,
        cost_estimate=pl.CostEstimate(
            flops=flops, transcendentals=0, bytes_accessed=2 * root_iter.size * 4
        ),
    )(root_iter)


def transforms(cols_t, departure, weight):
    members = cols_t.shape[2]
    highest = lax.Precision.HIGH
    scaled = cols_t * weight[:, :, None]
    gram_mat = jnp.einsum("bpk,bpj->bkj", scaled, cols_t, precision=highest)
    identity = jnp.eye(members, dtype=jnp.float32)
    system = gram_mat + (members - 1.0) * identity[None]
    half_trace = 0.5 * jnp.trace(system, axis1=1, axis2=2)
    root_iter = system / half_trace[:, None, None]
    inv_root = newton_schulz(root_iter)
    covariance = (
        jnp.einsum("bij,bjk->bik", inv_root, inv_root, precision=highest)
        / half_trace[:, None, None]
    )
    pulled = jnp.einsum("bpk,bp->bk", scaled, departure, precision=highest)
    mean_shift = jnp.einsum("bij,bj->bi", covariance, pulled, precision=highest)
    spread = inv_root * jnp.sqrt((members - 1.0) / half_trace)[:, None, None]
    return (spread + mean_shift[:, :, None]).astype(jnp.bfloat16)


def analyse(fields, weights_tot, n_dest):
    members, levels, span_cols = fields.shape
    blocks = weights_tot.shape[0]
    average = jnp.mean(fields.astype(jnp.float32), axis=0)
    perturb = (fields.astype(jnp.float32) - average[None]).astype(jnp.bfloat16)
    blocked = perturb.reshape(members, levels, blocks, span_cols // blocks)
    w_split = weights_tot.reshape(blocks, members, n_dest, members // n_dest)
    increment = jnp.einsum(
        "klbc,bkdn->dnlbc", blocked, w_split, preferred_element_type=jnp.float32
    )
    increment = increment.reshape(n_dest, members // n_dest, levels, span_cols)
    return (increment + average[None, None]).astype(jnp.bfloat16)


def per_device(background, obs_ens, observed, variance, obs_slot, obs_count, loc_bin):
    n_y = lax.axis_size("my")
    n_x = lax.axis_size("mx")
    n_c = lax.axis_size("mc")
    n_m = n_y * n_x * n_c
    n_s = lax.axis_size("space")
    k_loc, levels, span = background.shape
    members = k_loc * n_m
    chunk = span // n_m
    blk_loc, n_slot = obs_slot.shape[1], obs_slot.shape[2]

    send_bg = background.reshape(k_loc, levels, n_m, chunk).transpose(2, 0, 1, 3)

    me_y = lax.axis_index("my")
    slots_own = obs_slot[0].reshape(-1)
    shifted = [slots_own]
    for d in range(1, n_y):
        shifted.append(lax.ppermute(slots_own, "my", [(i, (i + d) % n_y) for i in range(n_y)]))
    shifted = jnp.stack(shifted)
    slots_grp = shifted.at[(me_y - jnp.arange(n_y)) % n_y].get(mode="promise_in_bounds")

    rows = jnp.concatenate([obs_ens, observed[None], variance[None]], axis=0)
    up = [(i, (i + 1) % n_s) for i in range(n_s)]
    down = [((i + 1) % n_s, i) for i in range(n_s)]
    before = lax.ppermute(rows, "space", up)
    after = lax.ppermute(rows, "space", down)
    near = jnp.concatenate([before, rows, after], axis=1)
    obs_cols = near[k_loc].at[slots_own].get(mode="promise_in_bounds").reshape(blk_loc, n_slot)
    var_cols = near[k_loc + 1].at[slots_own].get(mode="promise_in_bounds").reshape(blk_loc, n_slot)
    n_near = near.shape[1]

    group_t = lax.all_gather(near[:k_loc].T, ("mx", "mc"), axis=1, tiled=True)

    obs_cols, var_cols, send_bg = lax.optimization_barrier((obs_cols, var_cols, send_bg))
    fields = lax.all_to_all(send_bg, MEMBER, 0, 0, tiled=True).reshape(members, levels, chunk)

    picked = jnp.take(group_t, slots_grp.reshape(-1), axis=0, mode="clip")
    picked, fields = lax.optimization_barrier((picked, fields))
    send = picked.reshape(n_y, blk_loc * n_slot, n_x * n_c * k_loc)
    recv = lax.all_to_all(send, "my", 0, 0, tiled=True)
    ens_cols = recv.transpose(1, 0, 2).reshape(blk_loc, n_slot, members)

    obs_mean = jnp.mean(ens_cols, axis=2)
    cols_t = ens_cols - obs_mean[:, :, None]
    dep_cols = obs_cols - obs_mean
    in_range = jnp.arange(n_slot, dtype=jnp.int32)[None, :] < obs_count[0][:, None]
    weight = jnp.where(in_range, localize(loc_bin[0]) / var_cols, 0.0)
    weights_tot = transforms(cols_t, dep_cols, weight)

    send_out = analyse(fields, weights_tot, n_m)
    back = lax.all_to_all(send_out, MEMBER, 0, 0, tiled=True)
    return back.transpose(1, 2, 0, 3).reshape(k_loc, levels, span)


def solution(mesh):
    devs = mesh.devices
    n_m, n_s = devs.shape
    n_c = 2
    n_y = n_m // (n_c * 4)
    mesh3 = Mesh(devs.reshape(n_y, n_m // (n_y * n_c), n_c, n_s), ("my", "mx", "mc", "space"))
    in_specs = (
        P(MEMBER, None, "space"),
        P(MEMBER, "space"),
        P("space"),
        P("space"),
        P("space", MEMBER, None),
        P("space", MEMBER),
        P("space", MEMBER, None),
    )
    out_specs = P(MEMBER, None, "space")
    return jax.shard_map(
        per_device, mesh=mesh3, in_specs=in_specs, out_specs=out_specs, check_vma=False
    )
```

```python
import jax
import jax.numpy as jnp
from jax import lax
from jax.sharding import Mesh, PartitionSpec as P
from jax.experimental import pallas as pl
from jax.experimental.pallas import tpu as pltpu

ITERS = 8
NBINS = 32
MEMBER = ("my", "mx", "mc")


def localize(bin_idx):
    scaled = bin_idx.astype(jnp.float32) / (NBINS * 0.375)
    return jnp.exp(-0.5 * scaled * scaled)


def _split_dot(p, q):
    p_hi = p.astype(jnp.bfloat16)
    p_lo = (p - p_hi.astype(jnp.float32)).astype(jnp.bfloat16)
    q_hi = q.astype(jnp.bfloat16)
    q_lo = (q - q_hi.astype(jnp.float32)).astype(jnp.bfloat16)
    out = jnp.dot(p_hi, q_hi, preferred_element_type=jnp.float32)
    out = out + jnp.dot(p_hi, q_lo, preferred_element_type=jnp.float32)
    return out + jnp.dot(p_lo, q_hi, preferred_element_type=jnp.float32)


def _ns_kernel(root_ref, inv_ref):
    blocks, size = root_ref.shape[0], root_ref.shape[1]
    rows = lax.broadcasted_iota(jnp.int32, (size, size), 0)
    cols = lax.broadcasted_iota(jnp.int32, (size, size), 1)
    eye = (rows == cols).astype(jnp.float32)
    root = [root_ref[b] for b in range(blocks)]
    correct = [1.5 * eye - 0.5 * r for r in root]
    root = [_split_dot(c, r) for c, r in zip(correct, root)]
    inv = correct
    for sweep_num in range(1, ITERS):
        correct = [1.5 * eye - 0.5 * _split_dot(z, r) for z, r in zip(inv, root)]
        both = [
            _split_dot(c, jnp.concatenate([r, z], axis=1)) for c, r, z in zip(correct, root, inv)
        ]
        root = [x[:, :size] for x in both]
        inv = [x[:, size:] for x in both]
    for b in range(blocks):
        inv_ref[b] = inv[b]


def newton_schulz(root_iter):
    blocks, size, _ = root_iter.shape
    flops = blocks * (ITERS * 3 - 1) * 3 * 2 * size ** 3
    return pl.pallas_call(
        _ns_kernel,
        out_shape=jax.ShapeDtypeStruct(root_iter.shape, jnp.float32),
        in_specs=[pl.BlockSpec(memory_space=pltpu.VMEM)],
        out_specs=pl.BlockSpec(memory_space=pltpu.VMEM),
        cost_estimate=pl.CostEstimate(
            flops=flops, transcendentals=0, bytes_accessed=2 * root_iter.size * 4
        ),
    )(root_iter)


def transforms(cols_t, departure, weight):
    members = cols_t.shape[2]
    highest = lax.Precision.HIGH
    scaled = cols_t * weight[:, :, None]
    gram_mat = jnp.einsum("bpk,bpj->bkj", scaled, cols_t, precision=highest)
    identity = jnp.eye(members, dtype=jnp.float32)
    system = gram_mat + (members - 1.0) * identity[None]
    half_trace = 0.5 * jnp.trace(system, axis1=1, axis2=2)
    root_iter = system / half_trace[:, None, None]
    inv_root = newton_schulz(root_iter)
    covariance = (
        jnp.einsum("bij,bjk->bik", inv_root, inv_root, precision=highest)
        / half_trace[:, None, None]
    )
    pulled = jnp.einsum("bpk,bp->bk", scaled, departure, precision=highest)
    mean_shift = jnp.einsum("bij,bj->bi", covariance, pulled, precision=highest)
    spread = inv_root * jnp.sqrt((members - 1.0) / half_trace)[:, None, None]
    return (spread + mean_shift[:, :, None]).astype(jnp.bfloat16)


def analyse(fields, weights_tot, n_dest):
    members, levels, span_cols = fields.shape
    blocks = weights_tot.shape[0]
    average = jnp.mean(fields.astype(jnp.float32), axis=0)
    perturb = (fields.astype(jnp.float32) - average[None]).astype(jnp.bfloat16)
    blocked = perturb.reshape(members, levels, blocks, span_cols // blocks)
    w_split = weights_tot.reshape(blocks, members, n_dest, members // n_dest)
    increment = jnp.einsum(
        "klbc,bkdn->dnlbc", blocked, w_split, preferred_element_type=jnp.float32
    )
    increment = increment.reshape(n_dest, members // n_dest, levels, span_cols)
    return (increment + average[None, None]).astype(jnp.bfloat16)


def per_device(background, obs_ens, observed, variance, obs_slot, obs_count, loc_bin):
    n_y = lax.axis_size("my")
    n_x = lax.axis_size("mx")
    n_c = lax.axis_size("mc")
    n_m = n_y * n_x * n_c
    n_s = lax.axis_size("space")
    k_loc, levels, span = background.shape
    members = k_loc * n_m
    chunk = span // n_m
    blk_loc, n_slot = obs_slot.shape[1], obs_slot.shape[2]

    send_bg = background.reshape(k_loc, levels, n_m, chunk).transpose(2, 0, 1, 3)

    me_y = lax.axis_index("my")
    slots_own = obs_slot[0].reshape(-1)
    shifted = [slots_own]
    for d in range(1, n_y):
        shifted.append(lax.ppermute(slots_own, "my", [(i, (i + d) % n_y) for i in range(n_y)]))
    shifted = jnp.stack(shifted)
    slots_grp = shifted.at[(me_y - jnp.arange(n_y)) % n_y].get(mode="promise_in_bounds")

    rows = jnp.concatenate([obs_ens, observed[None], variance[None]], axis=0)
    up = [(i, (i + 1) % n_s) for i in range(n_s)]
    down = [((i + 1) % n_s, i) for i in range(n_s)]
    before = lax.ppermute(rows, "space", up)
    after = lax.ppermute(rows, "space", down)
    near = jnp.concatenate([before, rows, after], axis=1)
    obs_cols = near[k_loc].at[slots_own].get(mode="promise_in_bounds").reshape(blk_loc, n_slot)
    var_cols = near[k_loc + 1].at[slots_own].get(mode="promise_in_bounds").reshape(blk_loc, n_slot)
    n_near = near.shape[1]

    group_t = lax.all_gather(near[:k_loc].T, ("mx", "mc"), axis=1, tiled=True)

    obs_cols, var_cols, send_bg = lax.optimization_barrier((obs_cols, var_cols, send_bg))
    fields = lax.all_to_all(send_bg, MEMBER, 0, 0, tiled=True).reshape(members, levels, chunk)

    picked = jnp.take(group_t, slots_grp.reshape(-1), axis=0, mode="clip")
    picked, fields = lax.optimization_barrier((picked, fields))
    send = picked.reshape(n_y, blk_loc * n_slot, n_x * n_c * k_loc)
    recv = lax.all_to_all(send, "my", 0, 0, tiled=True)
    ens_cols = recv.transpose(1, 0, 2).reshape(blk_loc, n_slot, members)

    obs_mean = jnp.mean(ens_cols, axis=2)
    cols_t = ens_cols - obs_mean[:, :, None]
    dep_cols = obs_cols - obs_mean
    in_range = jnp.arange(n_slot, dtype=jnp.int32)[None, :] < obs_count[0][:, None]
    weight = jnp.where(in_range, localize(loc_bin[0]) / var_cols, 0.0)
    weights_tot = transforms(cols_t, dep_cols, weight)

    send_out = analyse(fields, weights_tot, n_m)
    back = lax.all_to_all(send_out, MEMBER, 0, 0, tiled=True)
    return back.transpose(1, 2, 0, 3).reshape(k_loc, levels, span)


def solution(mesh):
    devs = mesh.devices
    n_m, n_s = devs.shape
    n_c = 2
    n_y = n_m // (n_c * 4)
    mesh3 = Mesh(devs.reshape(n_y, n_m // (n_y * n_c), n_c, n_s), ("my", "mx", "mc", "space"))
    in_specs = (
        P(MEMBER, None, "space"),
        P(MEMBER, "space"),
        P("space"),
        P("space"),
        P("space", MEMBER, None),
        P("space", MEMBER),
        P("space", MEMBER, None),
    )
    out_specs = P(MEMBER, None, "space")
    return jax.shard_map(
        per_device, mesh=mesh3, in_specs=in_specs, out_specs=out_specs, check_vma=False
    )
```

```python
import jax
import jax.numpy as jnp
from jax import lax
from jax.sharding import Mesh, PartitionSpec as P
from jax.experimental import pallas as pl
from jax.experimental.pallas import tpu as pltpu

ITERS = 8
NBINS = 32
MEMBER = ("my", "mx", "mc")


def localize(bin_idx):
    scaled = bin_idx.astype(jnp.float32) / (NBINS * 0.375)
    return jnp.exp(-0.5 * scaled * scaled)


def _split_dot(p, q):
    p_hi = p.astype(jnp.bfloat16)
    p_lo = (p - p_hi.astype(jnp.float32)).astype(jnp.bfloat16)
    q_hi = q.astype(jnp.bfloat16)
    q_lo = (q - q_hi.astype(jnp.float32)).astype(jnp.bfloat16)
    out = jnp.dot(p_hi, q_hi, preferred_element_type=jnp.float32)
    out = out + jnp.dot(p_hi, q_lo, preferred_element_type=jnp.float32)
    return out + jnp.dot(p_lo, q_hi, preferred_element_type=jnp.float32)


def _ns_kernel(root_ref, inv_ref):
    blocks, size = root_ref.shape[0], root_ref.shape[1]
    rows = lax.broadcasted_iota(jnp.int32, (size, size), 0)
    cols = lax.broadcasted_iota(jnp.int32, (size, size), 1)
    eye = (rows == cols).astype(jnp.float32)
    root = [root_ref[b] for b in range(blocks)]
    correct = [1.5 * eye - 0.5 * r for r in root]
    root = [_split_dot(c, r) for c, r in zip(correct, root)]
    inv = correct
    for sweep_num in range(1, ITERS):
        correct = [1.5 * eye - 0.5 * _split_dot(z, r) for z, r in zip(inv, root)]
        both = [
            _split_dot(c, jnp.concatenate([r, z], axis=1)) for c, r, z in zip(correct, root, inv)
        ]
        root = [x[:, :size] for x in both]
        inv = [x[:, size:] for x in both]
    for b in range(blocks):
        inv_ref[b] = inv[b]


def newton_schulz(root_iter):
    blocks, size, _ = root_iter.shape
    flops = blocks * (ITERS * 3 - 1) * 3 * 2 * size ** 3
    return pl.pallas_call(
        _ns_kernel,
        out_shape=jax.ShapeDtypeStruct(root_iter.shape, jnp.float32),
        in_specs=[pl.BlockSpec(memory_space=pltpu.VMEM)],
        out_specs=pl.BlockSpec(memory_space=pltpu.VMEM),
        cost_estimate=pl.CostEstimate(
            flops=flops, transcendentals=0, bytes_accessed=2 * root_iter.size * 4
        ),
    )(root_iter)


def transforms(cols_t, departure, weight):
    members = cols_t.shape[2]
    highest = lax.Precision.HIGH
    scaled = cols_t * weight[:, :, None]
    gram_mat = jnp.einsum("bpk,bpj->bkj", scaled, cols_t, precision=highest)
    identity = jnp.eye(members, dtype=jnp.float32)
    system = gram_mat + (members - 1.0) * identity[None]
    half_trace = 0.5 * jnp.trace(system, axis1=1, axis2=2)
    root_iter = system / half_trace[:, None, None]
    inv_root = newton_schulz(root_iter)
    covariance = (
        jnp.einsum("bij,bjk->bik", inv_root, inv_root, precision=highest)
        / half_trace[:, None, None]
    )
    pulled = jnp.einsum("bpk,bp->bk", scaled, departure, precision=highest)
    mean_shift = jnp.einsum("bij,bj->bi", covariance, pulled, precision=highest)
    spread = inv_root * jnp.sqrt((members - 1.0) / half_trace)[:, None, None]
    return (spread + mean_shift[:, :, None]).astype(jnp.bfloat16)


def analyse(fields, weights_tot, n_dest):
    members, levels, span_cols = fields.shape
    blocks = weights_tot.shape[0]
    average = jnp.mean(fields.astype(jnp.float32), axis=0)
    perturb = (fields.astype(jnp.float32) - average[None]).astype(jnp.bfloat16)
    blocked = perturb.reshape(members, levels, blocks, span_cols // blocks)
    w_split = weights_tot.reshape(blocks, members, n_dest, members // n_dest)
    increment = jnp.einsum(
        "klbc,bkdn->dnlbc", blocked, w_split, preferred_element_type=jnp.float32
    )
    increment = increment.reshape(n_dest, members // n_dest, levels, span_cols)
    return (increment + average[None, None]).astype(jnp.bfloat16)


def per_device(background, obs_ens, observed, variance, obs_slot, obs_count, loc_bin):
    n_y = lax.axis_size("my")
    n_x = lax.axis_size("mx")
    n_c = lax.axis_size("mc")
    n_m = n_y * n_x * n_c
    n_s = lax.axis_size("space")
    k_loc, levels, span = background.shape
    members = k_loc * n_m
    chunk = span // n_m
    blk_loc, n_slot = obs_slot.shape[1], obs_slot.shape[2]

    send_bg = background.reshape(k_loc, levels, n_m, chunk).transpose(2, 0, 1, 3)

    me_y = lax.axis_index("my")
    slots_own = obs_slot[0].reshape(-1)
    shifted = [slots_own]
    for d in range(1, n_y):
        shifted.append(lax.ppermute(slots_own, "my", [(i, (i + d) % n_y) for i in range(n_y)]))
    shifted = jnp.stack(shifted)
    slots_grp = shifted.at[(me_y - jnp.arange(n_y)) % n_y].get(mode="promise_in_bounds")

    rows = jnp.concatenate([obs_ens, observed[None], variance[None]], axis=0)
    up = [(i, (i + 1) % n_s) for i in range(n_s)]
    down = [((i + 1) % n_s, i) for i in range(n_s)]
    before = lax.ppermute(rows, "space", up)
    after = lax.ppermute(rows, "space", down)
    fields = lax.all_to_all(send_bg, MEMBER, 0, 0, tiled=True).reshape(members, levels, chunk)
    before, after, fields = lax.optimization_barrier((before, after, fields))
    near = jnp.concatenate([before, rows, after], axis=1)
    obs_cols = near[k_loc].at[slots_own].get(mode="promise_in_bounds").reshape(blk_loc, n_slot)
    var_cols = near[k_loc + 1].at[slots_own].get(mode="promise_in_bounds").reshape(blk_loc, n_slot)
    n_near = near.shape[1]

    group_t = lax.all_gather(near[:k_loc].T, ("mx", "mc"), axis=1, tiled=True)


    picked = jnp.take(group_t, slots_grp.reshape(-1), axis=0, mode="clip")
    send = picked.reshape(n_y, blk_loc * n_slot, n_x * n_c * k_loc)
    recv = lax.all_to_all(send, "my", 0, 0, tiled=True)
    ens_cols = recv.transpose(1, 0, 2).reshape(blk_loc, n_slot, members)

    obs_mean = jnp.mean(ens_cols, axis=2)
    cols_t = ens_cols - obs_mean[:, :, None]
    dep_cols = obs_cols - obs_mean
    in_range = jnp.arange(n_slot, dtype=jnp.int32)[None, :] < obs_count[0][:, None]
    weight = jnp.where(in_range, localize(loc_bin[0]) / var_cols, 0.0)
    weights_tot = transforms(cols_t, dep_cols, weight)

    send_out = analyse(fields, weights_tot, n_m)
    back = lax.all_to_all(send_out, MEMBER, 0, 0, tiled=True)
    return back.transpose(1, 2, 0, 3).reshape(k_loc, levels, span)


def solution(mesh):
    devs = mesh.devices
    n_m, n_s = devs.shape
    n_c = 2
    n_y = n_m // (n_c * 4)
    mesh3 = Mesh(devs.reshape(n_y, n_m // (n_y * n_c), n_c, n_s), ("my", "mx", "mc", "space"))
    in_specs = (
        P(MEMBER, None, "space"),
        P(MEMBER, "space"),
        P("space"),
        P("space"),
        P("space", MEMBER, None),
        P("space", MEMBER),
        P("space", MEMBER, None),
    )
    out_specs = P(MEMBER, None, "space")
    return jax.shard_map(
        per_device, mesh=mesh3, in_specs=in_specs, out_specs=out_specs, check_vma=False
    )
```

```python
import jax
import jax.numpy as jnp
from jax import lax
from jax.sharding import Mesh, PartitionSpec as P
from jax.experimental import pallas as pl
from jax.experimental.pallas import tpu as pltpu

ITERS = 8
NBINS = 32
MEMBER = ("my", "mx", "mc")


def localize(bin_idx):
    scaled = bin_idx.astype(jnp.float32) / (NBINS * 0.375)
    return jnp.exp(-0.5 * scaled * scaled)


def _split_dot(p, q):
    p_hi = p.astype(jnp.bfloat16)
    p_lo = (p - p_hi.astype(jnp.float32)).astype(jnp.bfloat16)
    q_hi = q.astype(jnp.bfloat16)
    q_lo = (q - q_hi.astype(jnp.float32)).astype(jnp.bfloat16)
    out = jnp.dot(p_hi, q_hi, preferred_element_type=jnp.float32)
    out = out + jnp.dot(p_hi, q_lo, preferred_element_type=jnp.float32)
    return out + jnp.dot(p_lo, q_hi, preferred_element_type=jnp.float32)


def _ns_kernel(root_ref, inv_ref):
    blocks, size = root_ref.shape[0], root_ref.shape[1]
    rows = lax.broadcasted_iota(jnp.int32, (size, size), 0)
    cols = lax.broadcasted_iota(jnp.int32, (size, size), 1)
    eye = (rows == cols).astype(jnp.float32)
    root = [root_ref[b] for b in range(blocks)]
    correct = [1.5 * eye - 0.5 * r for r in root]
    root = [_split_dot(c, r) for c, r in zip(correct, root)]
    inv = correct
    for _ in range(1, ITERS):
        correct = [1.5 * eye - 0.5 * _split_dot(z, r) for z, r in zip(inv, root)]
        both = [
            _split_dot(c, jnp.concatenate([r, z], axis=1)) for c, r, z in zip(correct, root, inv)
        ]
        root = [x[:, :size] for x in both]
        inv = [x[:, size:] for x in both]
    for b in range(blocks):
        inv_ref[b] = inv[b]


def newton_schulz(root_iter):
    blocks, size, _ = root_iter.shape
    flops = blocks * (ITERS * 3 - 1) * 3 * 2 * size ** 3
    return pl.pallas_call(
        _ns_kernel,
        out_shape=jax.ShapeDtypeStruct(root_iter.shape, jnp.float32),
        in_specs=[pl.BlockSpec(memory_space=pltpu.VMEM)],
        out_specs=pl.BlockSpec(memory_space=pltpu.VMEM),
        cost_estimate=pl.CostEstimate(
            flops=flops, transcendentals=0, bytes_accessed=2 * root_iter.size * 4
        ),
    )(root_iter)


def transforms(cols_t, departure, weight):
    members = cols_t.shape[2]
    highest = lax.Precision.HIGH
    scaled = cols_t * weight[:, :, None]
    gram_mat = jnp.einsum("bpk,bpj->bkj", scaled, cols_t, precision=highest)
    identity = jnp.eye(members, dtype=jnp.float32)
    system = gram_mat + (members - 1.0) * identity[None]
    half_trace = 0.5 * jnp.trace(system, axis1=1, axis2=2)
    root_iter = system / half_trace[:, None, None]
    inv_root = newton_schulz(root_iter)
    covariance = (
        jnp.einsum("bij,bjk->bik", inv_root, inv_root, precision=highest)
        / half_trace[:, None, None]
    )
    pulled = jnp.einsum("bpk,bp->bk", scaled, departure, precision=highest)
    mean_shift = jnp.einsum("bij,bj->bi", covariance, pulled, precision=highest)
    spread = inv_root * jnp.sqrt((members - 1.0) / half_trace)[:, None, None]
    return (spread + mean_shift[:, :, None]).astype(jnp.bfloat16)


def analyse(fields, weights_tot, n_dest):
    members, levels, span_cols = fields.shape
    blocks = weights_tot.shape[0]
    average = jnp.mean(fields.astype(jnp.float32), axis=0)
    perturb = (fields.astype(jnp.float32) - average[None]).astype(jnp.bfloat16)
    blocked = perturb.reshape(members, levels, blocks, span_cols // blocks)
    w_split = weights_tot.reshape(blocks, members, n_dest, members // n_dest)
    increment = jnp.einsum(
        "klbc,bkdn->dnlbc", blocked, w_split, preferred_element_type=jnp.float32
    )
    increment = increment.reshape(n_dest, members // n_dest, levels, span_cols)
    return (increment + average[None, None]).astype(jnp.bfloat16)


def per_device(background, obs_ens, observed, variance, obs_slot, obs_count, loc_bin):
    n_y = lax.axis_size("my")
    n_x = lax.axis_size("mx")
    n_c = lax.axis_size("mc")
    n_m = n_y * n_x * n_c
    n_s = lax.axis_size("space")
    k_loc, levels, span = background.shape
    members = k_loc * n_m
    chunk = span // n_m
    blk_loc, n_slot = obs_slot.shape[1], obs_slot.shape[2]

    send_bg = background.reshape(k_loc, levels, n_m, chunk).transpose(2, 0, 1, 3)

    me_y = lax.axis_index("my")
    slots_own = obs_slot[0].reshape(-1)
    shifted = [slots_own]
    for d in range(1, n_y):
        shifted.append(lax.ppermute(slots_own, "my", [(i, (i + d) % n_y) for i in range(n_y)]))
    shifted = jnp.stack(shifted)
    slots_grp = shifted.at[(me_y - jnp.arange(n_y)) % n_y].get(mode="promise_in_bounds")

    rows = jnp.concatenate([obs_ens, observed[None], variance[None]], axis=0)
    up = [(i, (i + 1) % n_s) for i in range(n_s)]
    down = [((i + 1) % n_s, i) for i in range(n_s)]
    before = lax.ppermute(rows, "space", up)
    after = lax.ppermute(rows, "space", down)
    fields = lax.all_to_all(send_bg, MEMBER, 0, 0, tiled=True)
    fields = fields.reshape(members, levels, chunk)
    before, after, fields = lax.optimization_barrier((before, after, fields))
    near = jnp.concatenate([before, rows, after], axis=1)
    obs_cols = near[k_loc].at[slots_own].get(mode="promise_in_bounds").reshape(blk_loc, n_slot)
    var_cols = near[k_loc + 1].at[slots_own].get(mode="promise_in_bounds").reshape(blk_loc, n_slot)

    group_t = lax.all_gather(near[:k_loc].T, ("mx", "mc"), axis=1, tiled=True)


    picked = jnp.take(group_t, slots_grp.reshape(-1), axis=0, mode="clip")
    send = picked.reshape(n_y, blk_loc * n_slot, n_x * n_c * k_loc)
    recv = lax.all_to_all(send, "my", 0, 0, tiled=True)
    ens_cols = recv.transpose(1, 0, 2).reshape(blk_loc, n_slot, members)

    obs_mean = jnp.mean(ens_cols, axis=2)
    cols_t = ens_cols - obs_mean[:, :, None]
    dep_cols = obs_cols - obs_mean
    in_range = jnp.arange(n_slot, dtype=jnp.int32)[None, :] < obs_count[0][:, None]
    weight = jnp.where(in_range, localize(loc_bin[0]) / var_cols, 0.0)
    weights_tot = transforms(cols_t, dep_cols, weight)

    send_out = analyse(fields, weights_tot, n_m)
    back = lax.all_to_all(send_out, MEMBER, 0, 0, tiled=True)
    return back.transpose(1, 2, 0, 3).reshape(k_loc, levels, span)


def solution(mesh):
    devs = mesh.devices
    n_m, n_s = devs.shape
    n_c = 2
    n_y = n_m // (n_c * 4)
    mesh3 = Mesh(devs.reshape(n_y, n_m // (n_y * n_c), n_c, n_s), ("my", "mx", "mc", "space"))
    in_specs = (
        P(MEMBER, None, "space"),
        P(MEMBER, "space"),
        P("space"),
        P("space"),
        P("space", MEMBER, None),
        P("space", MEMBER),
        P("space", MEMBER, None),
    )
    out_specs = P(MEMBER, None, "space")

    return jax.shard_map(
        per_device, mesh=mesh3, in_specs=in_specs, out_specs=out_specs, check_vma=False
    )
```

```python
import jax
import jax.numpy as jnp
from jax import lax
from jax.sharding import Mesh, PartitionSpec as P
from jax.experimental import pallas as pl
from jax.experimental.pallas import tpu as pltpu

ITERS = 8
NBINS = 32
MEMBER = ("my", "mx", "mc")


def localize(bin_idx):
    scaled = bin_idx.astype(jnp.float32) / (NBINS * 0.375)
    return jnp.exp(-0.5 * scaled * scaled)


def _split_dot(p, q, dims=(((1,), (0,)), ((), ()))):
    p_hi = p.astype(jnp.bfloat16)
    p_lo = (p - p_hi.astype(jnp.float32)).astype(jnp.bfloat16)
    q_hi = q.astype(jnp.bfloat16)
    q_lo = (q - q_hi.astype(jnp.float32)).astype(jnp.bfloat16)
    out = lax.dot_general(p_hi, q_hi, dims, preferred_element_type=jnp.float32)
    out = out + lax.dot_general(p_hi, q_lo, dims, preferred_element_type=jnp.float32)
    return out + lax.dot_general(p_lo, q_hi, dims, preferred_element_type=jnp.float32)


def _ns_kernel(root_ref, aux_ref, out_ref):
    blocks, size = root_ref.shape[0], root_ref.shape[1]
    rows = lax.broadcasted_iota(jnp.int32, (size, size), 0)
    cols = lax.broadcasted_iota(jnp.int32, (size, size), 1)
    eye = (rows == cols).astype(jnp.float32)
    root = [root_ref[b] for b in range(blocks)]
    correct = [1.5 * eye - 0.5 * r for r in root]
    root = [_split_dot(c, r) for c, r in zip(correct, root)]
    inv = correct
    for sweep_num in range(1, ITERS):
        correct = [1.5 * eye - 0.5 * _split_dot(z, r) for z, r in zip(inv, root)]
        both = [
            _split_dot(c, jnp.concatenate([r, z], axis=1)) for c, r, z in zip(correct, root, inv)
        ]
        root = [x[:, :size] for x in both]
        inv = [x[:, size:] for x in both]
    contract_last = (((1,), (1,)), ((), ()))
    for b in range(blocks):
        pulled = jnp.broadcast_to(aux_ref[b, 0:1, :], (size, size))
        half = aux_ref[b, 1:2, :]
        scale = aux_ref[b, 2:3, :]
        covariance = _split_dot(inv[b], inv[b]) / half
        mean_shift = _split_dot(covariance, pulled, contract_last)
        out_ref[b] = (inv[b] * scale + mean_shift).astype(out_ref.dtype)


def newton_schulz(root_iter, aux):
    blocks, size, _ = root_iter.shape
    flops = blocks * (ITERS * 3 + 1) * 3 * 2 * size ** 3
    return pl.pallas_call(
        _ns_kernel,
        out_shape=jax.ShapeDtypeStruct(root_iter.shape, jnp.bfloat16),
        in_specs=[pl.BlockSpec(memory_space=pltpu.VMEM)] * 2,
        out_specs=pl.BlockSpec(memory_space=pltpu.VMEM),
        cost_estimate=pl.CostEstimate(
            flops=flops, transcendentals=0, bytes_accessed=3 * root_iter.size * 4
        ),
    )(root_iter, aux)


def transforms(cols_t, departure, weight):
    members = cols_t.shape[2]
    highest = lax.Precision.HIGH
    scaled = cols_t * weight[:, :, None]
    gram_mat = jnp.einsum("bpk,bpj->bkj", scaled, cols_t, precision=highest)
    identity = jnp.eye(members, dtype=jnp.float32)
    system = gram_mat + (members - 1.0) * identity[None]
    half_trace = 0.5 * jnp.trace(system, axis1=1, axis2=2)
    root_iter = system / half_trace[:, None, None]
    pulled = jnp.einsum("bpk,bp->bk", scaled, departure, precision=highest)
    scale = jnp.sqrt((members - 1.0) / half_trace)
    rows = [pulled, jnp.broadcast_to(half_trace[:, None], pulled.shape),
            jnp.broadcast_to(scale[:, None], pulled.shape)]
    aux = jnp.concatenate(
        [jnp.stack(rows, axis=1), jnp.zeros((pulled.shape[0], 5, members), jnp.float32)], axis=1
    )
    return newton_schulz(root_iter, aux)


def analyse(fields, weights_tot, n_dest):
    members, levels, span_cols = fields.shape
    blocks = weights_tot.shape[0]
    average = jnp.mean(fields.astype(jnp.float32), axis=0)
    perturb = (fields.astype(jnp.float32) - average[None]).astype(jnp.bfloat16)
    blocked = perturb.reshape(members, levels, blocks, span_cols // blocks)
    w_split = weights_tot.reshape(blocks, members, n_dest, members // n_dest)
    increment = jnp.einsum(
        "klbc,bkdn->dnlbc", blocked, w_split, preferred_element_type=jnp.float32
    )
    increment = increment.reshape(n_dest, members // n_dest, levels, span_cols)
    return (increment + average[None, None]).astype(jnp.bfloat16)


def per_device(background, obs_ens, observed, variance, obs_slot, obs_count, loc_bin):
    n_y = lax.axis_size("my")
    n_x = lax.axis_size("mx")
    n_c = lax.axis_size("mc")
    n_m = n_y * n_x * n_c
    n_s = lax.axis_size("space")
    k_loc, levels, span = background.shape
    members = k_loc * n_m
    chunk = span // n_m
    blk_loc, n_slot = obs_slot.shape[1], obs_slot.shape[2]

    send_bg = background.reshape(k_loc, levels, n_m, chunk).transpose(2, 0, 1, 3)

    me_y = lax.axis_index("my")
    slots_own = obs_slot[0].reshape(-1)
    shifted = [slots_own]
    for d in range(1, n_y):
        shifted.append(lax.ppermute(slots_own, "my", [(i, (i + d) % n_y) for i in range(n_y)]))
    shifted = jnp.stack(shifted)
    slots_grp = shifted.at[(me_y - jnp.arange(n_y)) % n_y].get(mode="promise_in_bounds")

    rows = jnp.concatenate([obs_ens, observed[None], variance[None]], axis=0)
    up = [(i, (i + 1) % n_s) for i in range(n_s)]
    down = [((i + 1) % n_s, i) for i in range(n_s)]
    before = lax.ppermute(rows, "space", up)
    after = lax.ppermute(rows, "space", down)
    near = jnp.concatenate([before, rows, after], axis=1)
    obs_cols = near[k_loc].at[slots_own].get(mode="promise_in_bounds").reshape(blk_loc, n_slot)
    var_cols = near[k_loc + 1].at[slots_own].get(mode="promise_in_bounds").reshape(blk_loc, n_slot)
    n_near = near.shape[1]

    group_t = lax.all_gather(near[:k_loc].T, ("mx", "mc"), axis=1, tiled=True)

    obs_cols, var_cols, send_bg = lax.optimization_barrier((obs_cols, var_cols, send_bg))
    fields = lax.all_to_all(send_bg, MEMBER, 0, 0, tiled=True).reshape(members, levels, chunk)

    picked = jnp.take(group_t, slots_grp.reshape(-1), axis=0, mode="clip")
    picked, fields = lax.optimization_barrier((picked, fields))
    send = picked.reshape(n_y, blk_loc * n_slot, n_x * n_c * k_loc)
    recv = lax.all_to_all(send, "my", 0, 0, tiled=True)
    ens_cols = recv.transpose(1, 0, 2).reshape(blk_loc, n_slot, members)

    obs_mean = jnp.mean(ens_cols, axis=2)
    cols_t = ens_cols - obs_mean[:, :, None]
    dep_cols = obs_cols - obs_mean
    in_range = jnp.arange(n_slot, dtype=jnp.int32)[None, :] < obs_count[0][:, None]
    weight = jnp.where(in_range, localize(loc_bin[0]) / var_cols, 0.0)
    weights_tot = transforms(cols_t, dep_cols, weight)

    send_out = analyse(fields, weights_tot, n_m)
    back = lax.all_to_all(send_out, MEMBER, 0, 0, tiled=True)
    return back.transpose(1, 2, 0, 3).reshape(k_loc, levels, span)


def solution(mesh):
    devs = mesh.devices
    n_m, n_s = devs.shape
    n_c = 2
    n_y = n_m // (n_c * 4)
    mesh3 = Mesh(devs.reshape(n_y, n_m // (n_y * n_c), n_c, n_s), ("my", "mx", "mc", "space"))
    in_specs = (
        P(MEMBER, None, "space"),
        P(MEMBER, "space"),
        P("space"),
        P("space"),
        P("space", MEMBER, None),
        P("space", MEMBER),
        P("space", MEMBER, None),
    )
    out_specs = P(MEMBER, None, "space")
    return jax.shard_map(
        per_device, mesh=mesh3, in_specs=in_specs, out_specs=out_specs, check_vma=False
    )
```

```python
import jax
import jax.numpy as jnp
from jax import lax
from jax.sharding import Mesh, PartitionSpec as P
from jax.experimental import pallas as pl
from jax.experimental.pallas import tpu as pltpu

ITERS = 8
NBINS = 32
MEMBER = ("my", "mx", "mc")


def localize(bin_idx):
    scaled = bin_idx.astype(jnp.float32) / (NBINS * 0.375)
    return jnp.exp(-0.5 * scaled * scaled)


def _split_dot(p, q):
    p_hi = p.astype(jnp.bfloat16)
    p_lo = (p - p_hi.astype(jnp.float32)).astype(jnp.bfloat16)
    q_hi = q.astype(jnp.bfloat16)
    q_lo = (q - q_hi.astype(jnp.float32)).astype(jnp.bfloat16)
    out = jnp.dot(p_hi, q_hi, preferred_element_type=jnp.float32)
    out = out + jnp.dot(p_hi, q_lo, preferred_element_type=jnp.float32)
    return out + jnp.dot(p_lo, q_hi, preferred_element_type=jnp.float32)


def _ns_kernel(root_ref, inv_ref):
    blocks, size = root_ref.shape[0], root_ref.shape[1]
    rows = lax.broadcasted_iota(jnp.int32, (size, size), 0)
    cols = lax.broadcasted_iota(jnp.int32, (size, size), 1)
    eye = (rows == cols).astype(jnp.float32)
    root = [root_ref[b] for b in range(blocks)]
    correct = [1.5 * eye - 0.5 * r for r in root]
    root = [_split_dot(c, r) for c, r in zip(correct, root)]
    inv = correct
    for sweep_num in range(1, ITERS):
        correct = [1.5 * eye - 0.5 * _split_dot(z, r) for z, r in zip(inv, root)]
        both = [
            _split_dot(c, jnp.concatenate([r, z], axis=1)) for c, r, z in zip(correct, root, inv)
        ]
        root = [x[:, :size] for x in both]
        inv = [x[:, size:] for x in both]
    for b in range(blocks):
        inv_ref[b] = inv[b]


def newton_schulz(root_iter):
    blocks, size, _ = root_iter.shape
    flops = blocks * (ITERS * 3 - 1) * 3 * 2 * size ** 3
    return pl.pallas_call(
        _ns_kernel,
        out_shape=jax.ShapeDtypeStruct(root_iter.shape, jnp.float32),
        in_specs=[pl.BlockSpec(memory_space=pltpu.VMEM)],
        out_specs=pl.BlockSpec(memory_space=pltpu.VMEM),
        cost_estimate=pl.CostEstimate(
            flops=flops, transcendentals=0, bytes_accessed=2 * root_iter.size * 4
        ),
    )(root_iter)


def transforms(cols_t, departure, weight):
    members = cols_t.shape[2]
    highest = lax.Precision.HIGH
    scaled = cols_t * weight[:, :, None]
    gram_mat = jnp.einsum("bpk,bpj->bkj", scaled, cols_t, precision=highest)
    identity = jnp.eye(members, dtype=jnp.float32)
    system = gram_mat + (members - 1.0) * identity[None]
    half_trace = 0.5 * jnp.trace(system, axis1=1, axis2=2)
    root_iter = system / half_trace[:, None, None]
    inv_root = newton_schulz(root_iter)
    covariance = (
        jnp.einsum("bij,bjk->bik", inv_root, inv_root, precision=highest)
        / half_trace[:, None, None]
    )
    pulled = jnp.einsum("bpk,bp->bk", scaled, departure, precision=highest)
    mean_shift = jnp.einsum("bij,bj->bi", covariance, pulled, precision=highest)
    spread = inv_root * jnp.sqrt((members - 1.0) / half_trace)[:, None, None]
    return (spread + mean_shift[:, :, None]).astype(jnp.bfloat16)


def analyse(fields, weights_tot, n_dest):
    members, levels, span_cols = fields.shape
    blocks = weights_tot.shape[0]
    average = jnp.mean(fields.astype(jnp.float32), axis=0)
    perturb = (fields.astype(jnp.float32) - average[None]).astype(jnp.bfloat16)
    blocked = perturb.reshape(members, levels, blocks, span_cols // blocks)
    w_split = weights_tot.reshape(blocks, members, n_dest, members // n_dest)
    increment = jnp.einsum(
        "klbc,bkdn->dnlbc", blocked, w_split, preferred_element_type=jnp.float32
    )
    increment = increment.reshape(n_dest, members // n_dest, levels, span_cols)
    return (increment + average[None, None]).astype(jnp.bfloat16)


def per_device(background, obs_ens, observed, variance, obs_slot, obs_count, loc_bin):
    n_y = lax.axis_size("my")
    n_x = lax.axis_size("mx")
    n_c = lax.axis_size("mc")
    n_m = n_y * n_x * n_c
    n_s = lax.axis_size("space")
    k_loc, levels, span = background.shape
    members = k_loc * n_m
    chunk = span // n_m
    blk_loc, n_slot = obs_slot.shape[1], obs_slot.shape[2]

    send_bg = background.reshape(k_loc, levels, n_m, chunk).transpose(2, 0, 1, 3)

    me_y = lax.axis_index("my")
    slots_own = obs_slot[0].reshape(-1)
    shifted = [slots_own]
    for d in range(1, n_y):
        shifted.append(lax.ppermute(slots_own, "my", [(i, (i + d) % n_y) for i in range(n_y)]))
    shifted = jnp.stack(shifted)
    slots_grp = shifted.at[(me_y - jnp.arange(n_y)) % n_y].get(mode="promise_in_bounds")

    rows = jnp.concatenate([obs_ens, observed[None], variance[None]], axis=0)
    up = [(i, (i + 1) % n_s) for i in range(n_s)]
    down = [((i + 1) % n_s, i) for i in range(n_s)]
    before = lax.ppermute(rows, "space", up)
    after = lax.ppermute(rows, "space", down)
    near = jnp.concatenate([before, rows, after], axis=1)
    obs_cols = near[k_loc].at[slots_own].get(mode="promise_in_bounds").reshape(blk_loc, n_slot)
    var_cols = near[k_loc + 1].at[slots_own].get(mode="promise_in_bounds").reshape(blk_loc, n_slot)
    n_near = near.shape[1]

    group_t = lax.all_gather(near[:k_loc].T, ("mx", "mc"), axis=1, tiled=True)


    picked = jnp.take(group_t, slots_grp.reshape(-1), axis=0, mode="clip")
    picked, send_bg = lax.optimization_barrier((picked, send_bg))
    fields = lax.all_to_all(send_bg, MEMBER, 0, 0, tiled=True).reshape(members, levels, chunk)
    send = picked.reshape(n_y, blk_loc * n_slot, n_x * n_c * k_loc)
    recv = lax.all_to_all(send, "my", 0, 0, tiled=True)
    ens_cols = recv.transpose(1, 0, 2).reshape(blk_loc, n_slot, members)

    obs_mean = jnp.mean(ens_cols, axis=2)
    cols_t = ens_cols - obs_mean[:, :, None]
    dep_cols = obs_cols - obs_mean
    in_range = jnp.arange(n_slot, dtype=jnp.int32)[None, :] < obs_count[0][:, None]
    weight = jnp.where(in_range, localize(loc_bin[0]) / var_cols, 0.0)
    weights_tot = transforms(cols_t, dep_cols, weight)

    send_out = analyse(fields, weights_tot, n_m)
    back = lax.all_to_all(send_out, MEMBER, 0, 0, tiled=True)
    return back.transpose(1, 2, 0, 3).reshape(k_loc, levels, span)


def solution(mesh):
    devs = mesh.devices
    n_m, n_s = devs.shape
    n_c = 2
    n_y = n_m // (n_c * 4)
    mesh3 = Mesh(devs.reshape(n_y, n_m // (n_y * n_c), n_c, n_s), ("my", "mx", "mc", "space"))
    in_specs = (
        P(MEMBER, None, "space"),
        P(MEMBER, "space"),
        P("space"),
        P("space"),
        P("space", MEMBER, None),
        P("space", MEMBER),
        P("space", MEMBER, None),
    )
    out_specs = P(MEMBER, None, "space")
    return jax.shard_map(
        per_device, mesh=mesh3, in_specs=in_specs, out_specs=out_specs, check_vma=False
    )
```

```python
import jax
import jax.numpy as jnp
from jax import lax
from jax.sharding import Mesh, PartitionSpec as P
from jax.experimental import pallas as pl
from jax.experimental.pallas import tpu as pltpu

ITERS = 8
NBINS = 32
MEMBER = ("my", "mx", "mc")


def localize(bin_idx):
    scaled = bin_idx.astype(jnp.float32) / (NBINS * 0.375)
    return jnp.exp(-0.5 * scaled * scaled)


def _split_dot(p, q):
    p_hi = p.astype(jnp.bfloat16)
    p_lo = (p - p_hi.astype(jnp.float32)).astype(jnp.bfloat16)
    q_hi = q.astype(jnp.bfloat16)
    q_lo = (q - q_hi.astype(jnp.float32)).astype(jnp.bfloat16)
    out = jnp.dot(p_hi, q_hi, preferred_element_type=jnp.float32)
    out = out + jnp.dot(p_hi, q_lo, preferred_element_type=jnp.float32)
    return out + jnp.dot(p_lo, q_hi, preferred_element_type=jnp.float32)


def _ns_kernel(root_ref, inv_ref):
    blocks, size = root_ref.shape[0], root_ref.shape[1]
    rows = lax.broadcasted_iota(jnp.int32, (size, size), 0)
    cols = lax.broadcasted_iota(jnp.int32, (size, size), 1)
    eye = (rows == cols).astype(jnp.float32)
    root = [root_ref[b] for b in range(blocks)]
    correct = [1.5 * eye - 0.5 * r for r in root]
    root = [_split_dot(c, r) for c, r in zip(correct, root)]
    inv = correct
    for sweep_num in range(1, ITERS):
        correct = [1.5 * eye - 0.5 * _split_dot(z, r) for z, r in zip(inv, root)]
        both = [
            _split_dot(c, jnp.concatenate([r, z], axis=1)) for c, r, z in zip(correct, root, inv)
        ]
        root = [x[:, :size] for x in both]
        inv = [x[:, size:] for x in both]
    for b in range(blocks):
        inv_ref[b] = inv[b]


def newton_schulz(root_iter):
    blocks, size, _ = root_iter.shape
    flops = blocks * (ITERS * 3 - 1) * 3 * 2 * size ** 3
    return pl.pallas_call(
        _ns_kernel,
        out_shape=jax.ShapeDtypeStruct(root_iter.shape, jnp.float32),
        in_specs=[pl.BlockSpec(memory_space=pltpu.VMEM)],
        out_specs=pl.BlockSpec(memory_space=pltpu.VMEM),
        cost_estimate=pl.CostEstimate(
            flops=flops, transcendentals=0, bytes_accessed=2 * root_iter.size * 4
        ),
    )(root_iter)


def transforms(cols_t, departure, weight):
    members = cols_t.shape[2]
    highest = lax.Precision.HIGH
    scaled = cols_t * weight[:, :, None]
    gram_mat = jnp.einsum("bpk,bpj->bkj", scaled, cols_t, precision=highest)
    identity = jnp.eye(members, dtype=jnp.float32)
    system = gram_mat + (members - 1.0) * identity[None]
    half_trace = 0.5 * jnp.trace(system, axis1=1, axis2=2)
    root_iter = system / half_trace[:, None, None]
    inv_root = newton_schulz(root_iter)
    covariance = (
        jnp.einsum("bij,bjk->bik", inv_root, inv_root, precision=highest)
        / half_trace[:, None, None]
    )
    pulled = jnp.einsum("bpk,bp->bk", scaled, departure, precision=highest)
    mean_shift = jnp.einsum("bij,bj->bi", covariance, pulled, precision=highest)
    spread = inv_root * jnp.sqrt((members - 1.0) / half_trace)[:, None, None]
    return (spread + mean_shift[:, :, None]).astype(jnp.bfloat16)


def analyse(fields, weights_tot, n_dest):
    members, levels, span_cols = fields.shape
    blocks = weights_tot.shape[0]
    average = jnp.mean(fields.astype(jnp.float32), axis=0)
    perturb = (fields.astype(jnp.float32) - average[None]).astype(jnp.bfloat16)
    blocked = perturb.reshape(members, levels, blocks, span_cols // blocks)
    w_split = weights_tot.reshape(blocks, members, n_dest, members // n_dest)
    increment = jnp.einsum(
        "klbc,bkdn->dnlbc", blocked, w_split, preferred_element_type=jnp.float32
    )
    increment = increment.reshape(n_dest, members // n_dest, levels, span_cols)
    return (increment + average[None, None]).astype(jnp.bfloat16)


def per_device(background, obs_ens, observed, variance, obs_slot, obs_count, loc_bin):
    n_y = lax.axis_size("my")
    n_x = lax.axis_size("mx")
    n_c = lax.axis_size("mc")
    n_m = n_y * n_x * n_c
    n_s = lax.axis_size("space")
    k_loc, levels, span = background.shape
    members = k_loc * n_m
    chunk = span // n_m
    blk_loc, n_slot = obs_slot.shape[1], obs_slot.shape[2]

    send_bg = background.reshape(k_loc, levels, n_m, chunk).transpose(2, 0, 1, 3)

    me_y = lax.axis_index("my")
    slots_own = obs_slot[0].reshape(-1)
    shifted = [slots_own]
    for d in range(1, n_y):
        shifted.append(lax.ppermute(slots_own, "my", [(i, (i + d) % n_y) for i in range(n_y)]))
    shifted = jnp.stack(shifted)
    slots_grp = shifted.at[(me_y - jnp.arange(n_y)) % n_y].get(mode="promise_in_bounds")

    rows = jnp.concatenate([obs_ens, observed[None], variance[None]], axis=0)
    up = [(i, (i + 1) % n_s) for i in range(n_s)]
    down = [((i + 1) % n_s, i) for i in range(n_s)]
    before = lax.ppermute(rows, "space", up)
    after = lax.ppermute(rows, "space", down)
    near = jnp.concatenate([before, rows, after], axis=1)
    obs_cols = near[k_loc].at[slots_own].get(mode="promise_in_bounds").reshape(blk_loc, n_slot)
    var_cols = near[k_loc + 1].at[slots_own].get(mode="promise_in_bounds").reshape(blk_loc, n_slot)
    n_near = near.shape[1]

    group_t = lax.all_gather(near[:k_loc].T, ("mx", "mc"), axis=1, tiled=True)

    group_t, send_bg, obs_cols, var_cols = lax.optimization_barrier(
        (group_t, send_bg, obs_cols, var_cols)
    )
    fields = lax.all_to_all(send_bg, MEMBER, 0, 0, tiled=True).reshape(members, levels, chunk)

    picked = jnp.take(group_t, slots_grp.reshape(-1), axis=0, mode="clip")
    picked, fields = lax.optimization_barrier((picked, fields))
    send = picked.reshape(n_y, blk_loc * n_slot, n_x * n_c * k_loc)
    recv = lax.all_to_all(send, "my", 0, 0, tiled=True)
    ens_cols = recv.transpose(1, 0, 2).reshape(blk_loc, n_slot, members)

    obs_mean = jnp.mean(ens_cols, axis=2)
    cols_t = ens_cols - obs_mean[:, :, None]
    dep_cols = obs_cols - obs_mean
    in_range = jnp.arange(n_slot, dtype=jnp.int32)[None, :] < obs_count[0][:, None]
    weight = jnp.where(in_range, localize(loc_bin[0]) / var_cols, 0.0)
    weights_tot = transforms(cols_t, dep_cols, weight)

    send_out = analyse(fields, weights_tot, n_m)
    back = lax.all_to_all(send_out, MEMBER, 0, 0, tiled=True)
    return back.transpose(1, 2, 0, 3).reshape(k_loc, levels, span)


def solution(mesh):
    devs = mesh.devices
    n_m, n_s = devs.shape
    n_c = 2
    n_y = n_m // (n_c * 4)
    mesh3 = Mesh(devs.reshape(n_y, n_m // (n_y * n_c), n_c, n_s), ("my", "mx", "mc", "space"))
    in_specs = (
        P(MEMBER, None, "space"),
        P(MEMBER, "space"),
        P("space"),
        P("space"),
        P("space", MEMBER, None),
        P("space", MEMBER),
        P("space", MEMBER, None),
    )
    out_specs = P(MEMBER, None, "space")
    return jax.shard_map(
        per_device, mesh=mesh3, in_specs=in_specs, out_specs=out_specs, check_vma=False
    )
```

```python
import jax
import jax.numpy as jnp
from jax import lax
from jax.sharding import Mesh, PartitionSpec as P
from jax.experimental import pallas as pl
from jax.experimental.pallas import tpu as pltpu

ITERS = 8
NBINS = 32
MEMBER = ("my", "mx", "mc")


def localize(bin_idx):
    scaled = bin_idx.astype(jnp.float32) / (NBINS * 0.375)
    return jnp.exp(-0.5 * scaled * scaled)


def _split_dot(p, q):
    p_hi = p.astype(jnp.bfloat16)
    p_lo = (p - p_hi.astype(jnp.float32)).astype(jnp.bfloat16)
    q_hi = q.astype(jnp.bfloat16)
    q_lo = (q - q_hi.astype(jnp.float32)).astype(jnp.bfloat16)
    out = jnp.dot(p_hi, q_hi, preferred_element_type=jnp.float32)
    out = out + jnp.dot(p_hi, q_lo, preferred_element_type=jnp.float32)
    return out + jnp.dot(p_lo, q_hi, preferred_element_type=jnp.float32)


def _ns_kernel(root_ref, inv_ref):
    blocks, size = root_ref.shape[0], root_ref.shape[1]
    rows = lax.broadcasted_iota(jnp.int32, (size, size), 0)
    cols = lax.broadcasted_iota(jnp.int32, (size, size), 1)
    eye = (rows == cols).astype(jnp.float32)
    root = [root_ref[b] for b in range(blocks)]
    correct = [1.5 * eye - 0.5 * r for r in root]
    root = [_split_dot(c, r) for c, r in zip(correct, root)]
    inv = correct
    for sweep_num in range(1, ITERS):
        correct = [1.5 * eye - 0.5 * _split_dot(z, r) for z, r in zip(inv, root)]
        both = [
            _split_dot(c, jnp.concatenate([r, z], axis=1)) for c, r, z in zip(correct, root, inv)
        ]
        root = [x[:, :size] for x in both]
        inv = [x[:, size:] for x in both]
    for b in range(blocks):
        inv_ref[b] = inv[b]


def newton_schulz(root_iter):
    blocks, size, _ = root_iter.shape
    flops = blocks * (ITERS * 3 - 1) * 3 * 2 * size ** 3
    return pl.pallas_call(
        _ns_kernel,
        out_shape=jax.ShapeDtypeStruct(root_iter.shape, jnp.float32),
        in_specs=[pl.BlockSpec(memory_space=pltpu.VMEM)],
        out_specs=pl.BlockSpec(memory_space=pltpu.VMEM),
        cost_estimate=pl.CostEstimate(
            flops=flops, transcendentals=0, bytes_accessed=2 * root_iter.size * 4
        ),
    )(root_iter)


def transforms(cols_t, departure, weight):
    members = cols_t.shape[2]
    highest = lax.Precision.HIGH
    scaled = cols_t * weight[:, :, None]
    gram_mat = jnp.einsum("bpk,bpj->bkj", scaled, cols_t, precision=highest)
    identity = jnp.eye(members, dtype=jnp.float32)
    system = gram_mat + (members - 1.0) * identity[None]
    half_trace = 0.5 * jnp.trace(system, axis1=1, axis2=2)
    root_iter = system / half_trace[:, None, None]
    inv_root = newton_schulz(root_iter)
    covariance = (
        jnp.einsum("bij,bjk->bik", inv_root, inv_root, precision=highest)
        / half_trace[:, None, None]
    )
    pulled = jnp.einsum("bpk,bp->bk", scaled, departure, precision=highest)
    mean_shift = jnp.einsum("bij,bj->bi", covariance, pulled, precision=highest)
    spread = inv_root * jnp.sqrt((members - 1.0) / half_trace)[:, None, None]
    return (spread + mean_shift[:, :, None]).astype(jnp.bfloat16)


def analyse(fields, weights_tot, n_dest):
    members, levels, span_cols = fields.shape
    blocks = weights_tot.shape[0]
    average = jnp.mean(fields.astype(jnp.float32), axis=0)
    perturb = (fields.astype(jnp.float32) - average[None]).astype(jnp.bfloat16)
    blocked = perturb.reshape(members, levels, blocks, span_cols // blocks)
    w_split = weights_tot.reshape(blocks, members, n_dest, members // n_dest)
    increment = jnp.einsum(
        "klbc,bkdn->dnlbc", blocked, w_split, preferred_element_type=jnp.float32
    )
    increment = increment.reshape(n_dest, members // n_dest, levels, span_cols)
    return (increment + average[None, None]).astype(jnp.bfloat16)


def per_device(background, obs_ens, observed, variance, obs_slot, obs_count, loc_bin):
    n_y = lax.axis_size("my")
    n_x = lax.axis_size("mx")
    n_c = lax.axis_size("mc")
    n_m = n_y * n_x * n_c
    n_s = lax.axis_size("space")
    k_loc, levels, span = background.shape
    members = k_loc * n_m
    chunk = span // n_m
    blk_loc, n_slot = obs_slot.shape[1], obs_slot.shape[2]

    send_bg = background.reshape(k_loc, levels, n_m, chunk).transpose(2, 0, 1, 3)

    me_y = lax.axis_index("my")
    slots_own = obs_slot[0].reshape(-1)
    shifted = [slots_own]
    for d in range(1, n_y):
        shifted.append(lax.ppermute(slots_own, "my", [(i, (i + d) % n_y) for i in range(n_y)]))
    shifted = jnp.stack(shifted)
    slots_grp = shifted.at[(me_y - jnp.arange(n_y)) % n_y].get(mode="promise_in_bounds")

    rows = jnp.concatenate([obs_ens, observed[None], variance[None]], axis=0)
    up = [(i, (i + 1) % n_s) for i in range(n_s)]
    down = [((i + 1) % n_s, i) for i in range(n_s)]
    before = lax.ppermute(rows, "space", up)
    after = lax.ppermute(rows, "space", down)
    near = jnp.concatenate([before, rows, after], axis=1)
    obs_cols = near[k_loc].at[slots_own].get(mode="promise_in_bounds").reshape(blk_loc, n_slot)
    var_cols = near[k_loc + 1].at[slots_own].get(mode="promise_in_bounds").reshape(blk_loc, n_slot)
    n_near = near.shape[1]

    group_t = lax.all_gather(near[:k_loc].T, ("mx", "mc"), axis=1, tiled=True)

    group_t, send_bg, obs_cols, var_cols, slots_grp = lax.optimization_barrier(
        (group_t, send_bg, obs_cols, var_cols, slots_grp)
    )
    fields = lax.all_to_all(send_bg, MEMBER, 0, 0, tiled=True).reshape(members, levels, chunk)

    picked = jnp.take(group_t, slots_grp.reshape(-1), axis=0, mode="clip")
    picked, fields = lax.optimization_barrier((picked, fields))
    send = picked.reshape(n_y, blk_loc * n_slot, n_x * n_c * k_loc)
    recv = lax.all_to_all(send, "my", 0, 0, tiled=True)
    ens_cols = recv.transpose(1, 0, 2).reshape(blk_loc, n_slot, members)

    obs_mean = jnp.mean(ens_cols, axis=2)
    cols_t = ens_cols - obs_mean[:, :, None]
    dep_cols = obs_cols - obs_mean
    in_range = jnp.arange(n_slot, dtype=jnp.int32)[None, :] < obs_count[0][:, None]
    weight = jnp.where(in_range, localize(loc_bin[0]) / var_cols, 0.0)
    weights_tot = transforms(cols_t, dep_cols, weight)

    send_out = analyse(fields, weights_tot, n_m)
    back = lax.all_to_all(send_out, MEMBER, 0, 0, tiled=True)
    return back.transpose(1, 2, 0, 3).reshape(k_loc, levels, span)


def solution(mesh):
    devs = mesh.devices
    n_m, n_s = devs.shape
    n_c = 2
    n_y = n_m // (n_c * 4)
    mesh3 = Mesh(devs.reshape(n_y, n_m // (n_y * n_c), n_c, n_s), ("my", "mx", "mc", "space"))
    in_specs = (
        P(MEMBER, None, "space"),
        P(MEMBER, "space"),
        P("space"),
        P("space"),
        P("space", MEMBER, None),
        P("space", MEMBER),
        P("space", MEMBER, None),
    )
    out_specs = P(MEMBER, None, "space")
    return jax.shard_map(
        per_device, mesh=mesh3, in_specs=in_specs, out_specs=out_specs, check_vma=False
    )
```
